256 devices in a mesh: hours: 64 (over z_hi, x, y, core), blocks: 4 (over z_lo).
Axes of the slice: x: 4, y: 4, z: 8 (z_hi: 2, z_lo: 4; z = z_hi * 4 + z_lo), core: 2. Of those that a mesh axis runs over, the one named last changes fastest.
Arguments:
- spectra: float32 [64, 64, 3, 2, 2048], P('hours', 'blocks'), may hold values from -6 to 6
- validity: int32 [64, 64], P('hours', 'blocks'), may hold values from 0 to 1, as said below
Outputs:
- near_stack: float32 [4, 2, 2304, 256], P('blocks', None, 'hours')
- far_stack: float32 [4, 1152, 256], P('blocks', 'hours')
The draws below stay inside these ranges and needn't reach their ends.
Inputs may be any that keep to these rules, and one draw needn't show every extreme that they name: `validity`: 0 or 1; some stations are invalid in every hour.
All inputs are finite; a program needn't handle non-finite values.
Results may differ from the reference program's by a relative error of at most 0.0058.
Values may be sent and summed in bfloat16 or wider, within the bound.
No kernel may reach another device: no remote copies, remote signals or barrier semaphores. Data moves between devices by JAX's collectives and lax.ppermute only.
A program may use at most 64 MiB of HBM per device.

```python
import math
import jax
import jax.numpy as jnp
from jax import lax

FREQS = 2048
BAND = 128
LAGS = 256
COMPS = 3
SB = 16
STATIONS = 64
HOURS = 64
N_BLOCKS = 4


def draw_validity(key, part):
    first_key, second_key, third_key = jax.random.split(key, 3)
    hour_index = jnp.arange(HOURS, dtype=jnp.int32)[:, None]
    threshold = 20 + 44 * hour_index // max(HOURS - 1, 1)
    rolled = jax.random.randint(first_key, (HOURS, STATIONS), 0, 64)
    alive = rolled < threshold
    outage = jax.random.randint(second_key, (1, STATIONS), 0, 16) == 0
    chosen = jax.random.randint(third_key, (1, 1), 0, STATIONS)
    outage = outage | (jnp.arange(STATIONS, dtype=jnp.int32)[None, :] == chosen)
    return jnp.where(alive & jnp.logical_not(outage), 1, 0).astype(jnp.int32)


def levels(own_key, extent, pieces, low, largest):
    gain = 1.0
    for position, parts in pieces:
        steps = jax.random.uniform(jax.random.fold_in(jax.random.fold_in(own_key, 6), position), (parts,), jnp.float32, low / len(pieces), largest / len(pieces))
        gain = gain * jnp.repeat(jnp.exp(steps), extent[position] // parts).reshape((-1,) + (1,) * (len(extent) - 1 - position))
    return gain


def normal_values(key, shape, scale, most, shards=(), kind=jnp.bfloat16):
    values = jax.random.normal(key, shape, jnp.float32) * scale
    if len(shards) > 0:
        values = levels(key, shape, shards, -0.22, 0.18) * values
    return jnp.clip(values, min=-most, max=most).astype(kind)


def setup_inputs(seed: int = 0) -> dict:
    seeds = jax.random.split(jax.random.key(seed), 3)
    spectra = normal_values(seeds[0], (HOURS, STATIONS, COMPS, 2, FREQS), 1.0, 6.0, ((0, 64), (1, 4)), jnp.float32)
    validity = draw_validity(jax.random.fold_in(seeds[2], 71), 0)
    return {"spectra": spectra, "validity": validity}


EPSILON = 1e-06

def whiten(spectra, validity, band_width):
    hour_count, station_count, comp_count, part_count, freq_count = spectra.shape
    grouped = spectra.reshape(hour_count, station_count, comp_count, part_count, freq_count // band_width, band_width)
    band_power = lax.optimization_barrier(jnp.mean(grouped * grouped, axis=(3, 5), keepdims=True))
    valid_f = validity.astype(jnp.float32).reshape(hour_count, station_count, 1, 1, 1, 1)
    scaled = grouped * (valid_f / jnp.sqrt(band_power + EPSILON))
    return scaled.reshape(hour_count, station_count * comp_count, part_count, freq_count).astype(jnp.bfloat16)

def build_table(freq_count, lag_count):
    freq_index = jnp.arange(freq_count, dtype=jnp.int32)[:, None]
    lag_index = jnp.arange(lag_count, dtype=jnp.int32)[None, :] - lag_count // 2
    residue = freq_index * (lag_index + 2 * freq_count) % (2 * freq_count)
    angles = residue.astype(jnp.float32) * (math.pi / freq_count)
    amplitude = 8.0 / math.sqrt(freq_count)
    return jnp.concatenate([jnp.cos(angles) * amplitude, -jnp.sin(angles) * amplitude], 0).astype(jnp.bfloat16)

def cross_spectrum(row_block, col_block):
    row_real = row_block[..., :, None, 0, :].astype(jnp.float32)
    row_imag = row_block[..., :, None, 1, :].astype(jnp.float32)
    col_real = col_block[..., None, :, 0, :].astype(jnp.float32)
    col_imag = col_block[..., None, :, 1, :].astype(jnp.float32)
    real_part = row_real * col_real + row_imag * col_imag
    imag_part = row_imag * col_real - row_real * col_imag
    stacked_parts = jnp.stack([real_part, imag_part], -2)
    dims_shape = stacked_parts.shape
    return stacked_parts.reshape(dims_shape[:-4] + (dims_shape[-4] * dims_shape[-3], dims_shape[-2] * dims_shape[-1])).astype(jnp.bfloat16)

def expand(counts, comp_count):
    return jnp.repeat(jnp.repeat(counts, comp_count, 0), comp_count, 1).reshape(-1)

def reference(spectra, validity):
    white = whiten(spectra, validity, BAND)
    table = build_table(FREQS, LAGS).astype(jnp.float32)
    valid_f = validity.astype(jnp.float32)
    pair_counts = jnp.dot(valid_f.T, valid_f, precision=lax.Precision.HIGHEST)
    trace_count = COMPS * SB
    half_width = trace_count // 2
    block_count = N_BLOCKS
    near_rounds = block_count // 2

    def stacked(row_start, row_count, col_start):
        row_block = white[:, row_start:row_start + row_count]
        col_block = white[:, col_start:col_start + trace_count]

        def add_hour(running, hour_pair):
            return (running + cross_spectrum(hour_pair[0], hour_pair[1]).astype(jnp.float32), None)
        running, unused = lax.scan(add_hour, jnp.zeros((row_count * trace_count, 2 * FREQS), jnp.float32), (row_block, col_block))
        correlogram = jnp.dot(running, table, precision=lax.Precision.HIGHEST)
        sub_block = pair_counts[row_start // COMPS:(row_start + row_count) // COMPS, col_start // COMPS:col_start // COMPS + SB]
        valid_hours = expand(sub_block, COMPS)
        return correlogram / jnp.maximum(valid_hours, 1.0)[:, None]
    near_list = []
    far_list = []
    for my_block in range(block_count):
        near_list.append(jnp.stack([stacked(my_block * trace_count, trace_count, (my_block - round_index) % block_count * trace_count) for round_index in range(near_rounds)], 0))
        partner = (my_block + near_rounds) % block_count
        if my_block < near_rounds:
            far_list.append(stacked(my_block * trace_count, half_width, partner * trace_count))
        else:
            far_list.append(stacked(partner * trace_count + half_width, half_width, my_block * trace_count))
    return (jnp.stack(near_list, 0), jnp.stack(far_list, 0))
```

```python
import math

import jax
import jax.numpy as jnp
from jax import lax
from jax.sharding import PartitionSpec as P

BAND = 128
LAGS = 256


EPSILON = 1e-06


def passed_along(block, axis, distance):
    devices = range(lax.axis_size(axis))
    route = [((i - distance) % len(devices), i) for i in devices]
    return lax.ppermute(block, axis, route)


def whiten(spectra, validity, band_width):
    hour_count, station_count, comp_count, part_count, freq_count = spectra.shape
    grouped = spectra.reshape(
        hour_count, station_count, comp_count, part_count, freq_count // band_width, band_width
    )
    band_power = jnp.mean(grouped * grouped, axis=(3, 5), keepdims=True)
    valid_f = validity.astype(jnp.float32).reshape(hour_count, station_count, 1, 1, 1, 1)
    scaled = grouped * (valid_f / jnp.sqrt(band_power + EPSILON))
    return scaled.reshape(hour_count, station_count * comp_count, part_count, freq_count).astype(
        jnp.bfloat16
    )


def build_table(freq_count, lag_count):
    freq_index = jnp.arange(freq_count, dtype=jnp.int32)[:, None]
    lag_index = jnp.arange(lag_count, dtype=jnp.int32)[None, :] - lag_count // 2
    residue = freq_index * (lag_index + 2 * freq_count) % (2 * freq_count)
    angles = residue.astype(jnp.float32) * (math.pi / freq_count)
    amplitude = 8.0 / math.sqrt(freq_count)
    return jnp.concatenate([jnp.cos(angles) * amplitude, -jnp.sin(angles) * amplitude], 0).astype(
        jnp.bfloat16
    )


def cross_spectrum(row_block, col_block):
    row_real = row_block[..., :, None, 0, :].astype(jnp.float32)
    row_imag = row_block[..., :, None, 1, :].astype(jnp.float32)
    col_real = col_block[..., None, :, 0, :].astype(jnp.float32)
    col_imag = col_block[..., None, :, 1, :].astype(jnp.float32)
    real_part = row_real * col_real + row_imag * col_imag
    imag_part = row_imag * col_real - row_real * col_imag
    stacked_parts = jnp.stack([real_part, imag_part], -2)
    dims_shape = stacked_parts.shape
    return stacked_parts.reshape(
        dims_shape[:-4] + (dims_shape[-4] * dims_shape[-3], dims_shape[-2] * dims_shape[-1])
    ).astype(jnp.bfloat16)


def expand(counts, comp_count):
    return jnp.repeat(jnp.repeat(counts, comp_count, 0), comp_count, 1).reshape(-1)


def correlate(row_block, col_block, table):
    hour_count, row_count, part_count, freq_count = row_block.shape
    trace_count = col_block.shape[1]
    row_step = 4
    grouped = row_block.reshape(
        hour_count, row_count // row_step, row_step, part_count, freq_count
    ).transpose(1, 0, 2, 3, 4)

    def one_block(sub_rows):
        spectrum = cross_spectrum(sub_rows, col_block)
        return jnp.einsum("hpk,kl->pl", spectrum, table, preferred_element_type=jnp.float32)

    result = lax.map(one_block, grouped)
    return result.reshape(row_count * trace_count, table.shape[1])


def on_device(spectra, validity):
    hour_count, station_count, comp_count, part_count, freq_count = spectra.shape
    trace_count = station_count * comp_count
    half_width = trace_count // 2
    white = whiten(spectra, validity, BAND)
    table = build_table(freq_count, LAGS)
    valid_wire = validity.astype(jnp.bfloat16)
    block_count = lax.axis_size("blocks")
    near_rounds = block_count // 2
    my_block = lax.axis_index("blocks")
    is_lower = my_block < near_rounds
    panels = [(white, valid_wire)]
    for round_index in range(1, near_rounds + 1):
        panels.append(passed_along((white, valid_wire), "blocks", round_index))
    near_terms = jnp.stack(
        [correlate(white, panels[round_index][0], table) for round_index in range(near_rounds)], 0
    )
    far_white, far_valid = panels[near_rounds]
    far_rows = jnp.where(is_lower, white[:, :half_width], far_white[:, half_width:])
    far_cols = jnp.where(is_lower, far_white, white)
    far_terms = correlate(far_rows, far_cols, table)

    def trace_valid(valid):
        return jnp.repeat(valid.reshape(-1).astype(jnp.float32), comp_count)

    own_valid = trace_valid(valid_wire)
    near_pairs = jnp.stack(
        [
            (own_valid[:, None] * trace_valid(panels[round_index][1])[None, :]).reshape(-1)
            for round_index in range(near_rounds)
        ],
        0,
    )
    far_trace_valid = trace_valid(far_valid)
    far_row_valid = jnp.where(is_lower, own_valid[:half_width], far_trace_valid[half_width:])
    far_col_valid = jnp.where(is_lower, far_trace_valid, own_valid)
    far_pairs = (far_row_valid[:, None] * far_col_valid[None, :]).reshape(-1)

    hour_devices = lax.axis_size("hours")
    share_near = trace_count * trace_count // hour_devices
    share_far = half_width * trace_count // hour_devices
    lag_count = table.shape[1]
    near_slots = near_terms.reshape(near_rounds, hour_devices, share_near, lag_count).transpose(1, 0, 2, 3)
    far_slots = far_terms.reshape(hour_devices, share_far, lag_count)
    count_slots = jnp.concatenate(
        [
            near_pairs.reshape(near_rounds, hour_devices, share_near).transpose(1, 0, 2).reshape(hour_devices, -1),
            far_pairs.reshape(hour_devices, share_far),
        ],
        1,
    )
    row_count = near_rounds * share_near + share_far
    count_row = jnp.pad(count_slots, ((0, 0), (0, lag_count - row_count)))[:, None, :]
    outgoing = jnp.concatenate(
        [near_slots.reshape(hour_devices, near_rounds * share_near, lag_count), far_slots, count_row], 1
    )
    incoming = lax.all_to_all(outgoing, "hours", 0, 0, tiled=True)
    total = jnp.sum(incoming, axis=0)
    pair_counts = jnp.maximum(total[row_count, :row_count], 1.0)
    stacked = total[:row_count] / pair_counts[:, None]
    near_stack = stacked[: near_rounds * share_near].reshape(near_rounds, share_near, lag_count)
    far_stack = stacked[near_rounds * share_near :]
    return (near_stack[None], far_stack[None])


def solution(mesh):
    in_specs = (P("hours", "blocks", None, None, None), P("hours", "blocks"))
    out_specs = (P("blocks", None, "hours", None), P("blocks", "hours", None))
    return jax.shard_map(
        on_device, mesh=mesh, in_specs=in_specs, out_specs=out_specs, check_vma=False
    )
```

```python
import math

import jax
import jax.numpy as jnp
from jax import lax
from jax.experimental import pallas as pl
from jax.experimental.pallas import tpu as pltpu
from jax.sharding import PartitionSpec as P

BAND = 128
LAGS = 256


EPSILON = 1e-06


def passed_along(block, axis, distance):
    devices = range(lax.axis_size(axis))
    route = [((i - distance) % len(devices), i) for i in devices]
    return lax.ppermute(block, axis, route)


def whiten(spectra, validity, band_width):
    hour_count, station_count, comp_count, part_count, freq_count = spectra.shape
    grouped = spectra.reshape(
        hour_count, station_count, comp_count, part_count, freq_count // band_width, band_width
    )
    band_power = jnp.mean(grouped * grouped, axis=(3, 5), keepdims=True)
    valid_f = validity.astype(jnp.float32).reshape(hour_count, station_count, 1, 1, 1, 1)
    scaled = grouped * (valid_f / jnp.sqrt(band_power + EPSILON))
    return scaled.reshape(hour_count, station_count * comp_count, part_count, freq_count).astype(
        jnp.bfloat16
    )


def build_table(freq_count, lag_count):
    freq_index = jnp.arange(freq_count, dtype=jnp.int32)[:, None]
    lag_index = jnp.arange(lag_count, dtype=jnp.int32)[None, :] - lag_count // 2
    residue = freq_index * (lag_index + 2 * freq_count) % (2 * freq_count)
    angles = residue.astype(jnp.float32) * (math.pi / freq_count)
    amplitude = 8.0 / math.sqrt(freq_count)
    return jnp.concatenate([jnp.cos(angles) * amplitude, -jnp.sin(angles) * amplitude], 0).astype(
        jnp.bfloat16
    )


def cross_spectrum(row_block, col_block):
    row_real = row_block[..., :, None, 0, :].astype(jnp.float32)
    row_imag = row_block[..., :, None, 1, :].astype(jnp.float32)
    col_real = col_block[..., None, :, 0, :].astype(jnp.float32)
    col_imag = col_block[..., None, :, 1, :].astype(jnp.float32)
    real_part = row_real * col_real + row_imag * col_imag
    imag_part = row_imag * col_real - row_real * col_imag
    stacked_parts = jnp.stack([real_part, imag_part], -2)
    dims_shape = stacked_parts.shape
    return stacked_parts.reshape(
        dims_shape[:-4] + (dims_shape[-4] * dims_shape[-3], dims_shape[-2] * dims_shape[-1])
    ).astype(jnp.bfloat16)


def expand(counts, comp_count):
    return jnp.repeat(jnp.repeat(counts, comp_count, 0), comp_count, 1).reshape(-1)


def correlate_kernel(rows_ref, cols_ref, table_ref, out_ref, cross_ref):
    row_step = rows_ref.shape[0]
    col_count, wide = cols_ref.shape
    freq_count = wide // 2
    chunk = 256
    for start in range(0, freq_count, chunk):
        col_real = cols_ref[:, start : start + chunk]
        col_imag = cols_ref[:, freq_count + start : freq_count + start + chunk]
        for row in range(row_step):
            row_real = rows_ref[row : row + 1, start : start + chunk]
            row_imag = rows_ref[row : row + 1, freq_count + start : freq_count + start + chunk]
            real_part = row_real * col_real + row_imag * col_imag
            imag_part = row_imag * col_real - row_real * col_imag
            first = row * col_count
            cross_ref[first : first + col_count, start : start + chunk] = real_part.astype(jnp.bfloat16)
            cross_ref[first : first + col_count, freq_count + start : freq_count + start + chunk] = (
                imag_part.astype(jnp.bfloat16)
            )
    out_ref[...] = jnp.dot(cross_ref[...], table_ref[...], preferred_element_type=jnp.float32)


def correlate(row_block, col_block, table):
    hour_count, row_count, part_count, freq_count = row_block.shape
    trace_count = col_block.shape[1]
    wide = part_count * freq_count
    rows = row_block.reshape(row_count, wide).astype(jnp.float32)
    cols = col_block.reshape(trace_count, wide).astype(jnp.float32)
    lag_count = table.shape[1]
    row_step = 8
    return pl.pallas_call(
        correlate_kernel,
        grid=(row_count // row_step,),
        in_specs=[
            pl.BlockSpec((row_step, wide), lambda i: (i, 0)),
            pl.BlockSpec((trace_count, wide), lambda i: (0, 0)),
            pl.BlockSpec((wide, lag_count), lambda i: (0, 0)),
        ],
        out_specs=pl.BlockSpec((row_step * trace_count, lag_count), lambda i: (i, 0)),
        out_shape=jax.ShapeDtypeStruct((row_count * trace_count, lag_count), jnp.float32),
        scratch_shapes=[pltpu.VMEM((row_step * trace_count, wide), jnp.bfloat16)],
    )(rows, cols, table)


def on_device(spectra, validity):
    hour_count, station_count, comp_count, part_count, freq_count = spectra.shape
    trace_count = station_count * comp_count
    half_width = trace_count // 2
    white = whiten(spectra, validity, BAND)
    table = build_table(freq_count, LAGS)
    valid_wire = validity.astype(jnp.bfloat16)
    block_count = lax.axis_size("blocks")
    near_rounds = block_count // 2
    my_block = lax.axis_index("blocks")
    is_lower = my_block < near_rounds
    panels = [(white, valid_wire)]
    for round_index in range(1, near_rounds + 1):
        panels.append(passed_along((white, valid_wire), "blocks", round_index))
    near_terms = jnp.stack(
        [correlate(white, panels[round_index][0], table) for round_index in range(near_rounds)], 0
    )
    far_white, far_valid = panels[near_rounds]
    far_rows = jnp.where(is_lower, white[:, :half_width], far_white[:, half_width:])
    far_cols = jnp.where(is_lower, far_white, white)
    far_terms = correlate(far_rows, far_cols, table)

    def trace_valid(valid):
        return jnp.repeat(valid.reshape(-1).astype(jnp.float32), comp_count)

    own_valid = trace_valid(valid_wire)
    near_pairs = jnp.stack(
        [
            (own_valid[:, None] * trace_valid(panels[round_index][1])[None, :]).reshape(-1)
            for round_index in range(near_rounds)
        ],
        0,
    )
    far_trace_valid = trace_valid(far_valid)
    far_row_valid = jnp.where(is_lower, own_valid[:half_width], far_trace_valid[half_width:])
    far_col_valid = jnp.where(is_lower, far_trace_valid, own_valid)
    far_pairs = (far_row_valid[:, None] * far_col_valid[None, :]).reshape(-1)

    hour_devices = lax.axis_size("hours")
    share_near = trace_count * trace_count // hour_devices
    share_far = half_width * trace_count // hour_devices
    lag_count = table.shape[1]
    near_slots = near_terms.reshape(near_rounds, hour_devices, share_near, lag_count).transpose(1, 0, 2, 3)
    far_slots = far_terms.reshape(hour_devices, share_far, lag_count)
    count_slots = jnp.concatenate(
        [
            near_pairs.reshape(near_rounds, hour_devices, share_near).transpose(1, 0, 2).reshape(hour_devices, -1),
            far_pairs.reshape(hour_devices, share_far),
        ],
        1,
    )
    row_count = near_rounds * share_near + share_far
    count_row = jnp.pad(count_slots, ((0, 0), (0, lag_count - row_count)))[:, None, :]
    outgoing = jnp.concatenate(
        [near_slots.reshape(hour_devices, near_rounds * share_near, lag_count), far_slots, count_row], 1
    )
    incoming = lax.all_to_all(outgoing, "hours", 0, 0, tiled=True)
    total = jnp.sum(incoming, axis=0)
    pair_counts = jnp.maximum(total[row_count, :row_count], 1.0)
    stacked = total[:row_count] / pair_counts[:, None]
    near_stack = stacked[: near_rounds * share_near].reshape(near_rounds, share_near, lag_count)
    far_stack = stacked[near_rounds * share_near :]
    return (near_stack[None], far_stack[None])


def solution(mesh):
    in_specs = (P("hours", "blocks", None, None, None), P("hours", "blocks"))
    out_specs = (P("blocks", None, "hours", None), P("blocks", "hours", None))
    return jax.shard_map(
        on_device, mesh=mesh, in_specs=in_specs, out_specs=out_specs, check_vma=False
    )
```

```python
import math

import jax
import jax.numpy as jnp
from jax import lax
from jax.experimental import pallas as pl
from jax.experimental.pallas import tpu as pltpu
from jax.sharding import Mesh, PartitionSpec as P

BAND = 128
LAGS = 256


EPSILON = 1e-06


HOUR_AXES = ("z_hi", "x", "y", "core")
HOUR_SPLIT = (2, 4, 4, 2)
REDUCE_STAGES = ((("core",), 3), (("x", "y"), 1), (("z_hi",), 0))


def passed_along(block, axis, distance):
    devices = range(lax.axis_size(axis))
    route = [((i - distance) % len(devices), i) for i in devices]
    return lax.ppermute(block, axis, route)


def whiten(spectra, validity, band_width):
    hour_count, station_count, comp_count, part_count, freq_count = spectra.shape
    grouped = spectra.reshape(
        hour_count, station_count, comp_count, part_count, freq_count // band_width, band_width
    )
    band_power = jnp.mean(grouped * grouped, axis=(3, 5), keepdims=True)
    valid_f = validity.astype(jnp.float32).reshape(hour_count, station_count, 1, 1, 1, 1)
    scaled = grouped * (valid_f / jnp.sqrt(band_power + EPSILON))
    return scaled.reshape(hour_count, station_count * comp_count, part_count, freq_count).astype(
        jnp.bfloat16
    )


def build_table(freq_count, lag_count):
    freq_index = jnp.arange(freq_count, dtype=jnp.int32)[:, None]
    lag_index = jnp.arange(lag_count, dtype=jnp.int32)[None, :] - lag_count // 2
    residue = freq_index * (lag_index + 2 * freq_count) % (2 * freq_count)
    angles = residue.astype(jnp.float32) * (math.pi / freq_count)
    amplitude = 8.0 / math.sqrt(freq_count)
    return jnp.concatenate([jnp.cos(angles) * amplitude, -jnp.sin(angles) * amplitude], 0).astype(
        jnp.bfloat16
    )


def cross_spectrum(row_block, col_block):
    row_real = row_block[..., :, None, 0, :].astype(jnp.float32)
    row_imag = row_block[..., :, None, 1, :].astype(jnp.float32)
    col_real = col_block[..., None, :, 0, :].astype(jnp.float32)
    col_imag = col_block[..., None, :, 1, :].astype(jnp.float32)
    real_part = row_real * col_real + row_imag * col_imag
    imag_part = row_imag * col_real - row_real * col_imag
    stacked_parts = jnp.stack([real_part, imag_part], -2)
    dims_shape = stacked_parts.shape
    return stacked_parts.reshape(
        dims_shape[:-4] + (dims_shape[-4] * dims_shape[-3], dims_shape[-2] * dims_shape[-1])
    ).astype(jnp.bfloat16)


def expand(counts, comp_count):
    return jnp.repeat(jnp.repeat(counts, comp_count, 0), comp_count, 1).reshape(-1)


def correlate_kernel(rows_ref, cols_ref, table_ref, out_ref, cross_ref):
    row_step = rows_ref.shape[0]
    col_count, wide = cols_ref.shape
    freq_count = wide // 2
    chunk = 256
    for start in range(0, freq_count, chunk):
        col_real = cols_ref[:, start : start + chunk]
        col_imag = cols_ref[:, freq_count + start : freq_count + start + chunk]
        for row in range(row_step):
            row_real = rows_ref[row : row + 1, start : start + chunk]
            row_imag = rows_ref[row : row + 1, freq_count + start : freq_count + start + chunk]
            real_part = row_real * col_real + row_imag * col_imag
            imag_part = row_imag * col_real - row_real * col_imag
            first = row * col_count
            cross_ref[first : first + col_count, start : start + chunk] = real_part.astype(jnp.bfloat16)
            cross_ref[first : first + col_count, freq_count + start : freq_count + start + chunk] = (
                imag_part.astype(jnp.bfloat16)
            )
    out_ref[...] = jnp.dot(cross_ref[...], table_ref[...], preferred_element_type=jnp.float32)


def correlate(row_block, col_block, table):
    hour_count, row_count, part_count, freq_count = row_block.shape
    trace_count = col_block.shape[1]
    wide = part_count * freq_count
    rows = row_block.reshape(row_count, wide).astype(jnp.float32)
    cols = col_block.reshape(trace_count, wide).astype(jnp.float32)
    lag_count = table.shape[1]
    row_step = 8
    return pl.pallas_call(
        correlate_kernel,
        grid=(row_count // row_step,),
        in_specs=[
            pl.BlockSpec((row_step, wide), lambda i: (i, 0)),
            pl.BlockSpec((trace_count, wide), lambda i: (0, 0)),
            pl.BlockSpec((wide, lag_count), lambda i: (0, 0)),
        ],
        out_specs=pl.BlockSpec((row_step * trace_count, lag_count), lambda i: (i, 0)),
        out_shape=jax.ShapeDtypeStruct((row_count * trace_count, lag_count), jnp.float32),
        scratch_shapes=[pltpu.VMEM((row_step * trace_count, wide), jnp.bfloat16)],
    )(rows, cols, table)


def on_device(spectra, validity):
    hour_count, station_count, comp_count, part_count, freq_count = spectra.shape
    trace_count = station_count * comp_count
    half_width = trace_count // 2
    white = whiten(spectra, validity, BAND)
    table = build_table(freq_count, LAGS)
    valid_wire = validity.astype(jnp.bfloat16)
    block_count = lax.axis_size("blocks")
    near_rounds = block_count // 2
    my_block = lax.axis_index("blocks")
    is_lower = my_block < near_rounds
    panels = [(white, valid_wire)]
    for round_index in range(1, near_rounds + 1):
        panels.append(passed_along((white, valid_wire), "blocks", round_index))
    near_terms = jnp.stack(
        [correlate(white, panels[round_index][0], table) for round_index in range(near_rounds)], 0
    )
    far_white, far_valid = panels[near_rounds]
    far_rows = jnp.where(is_lower, white[:, :half_width], far_white[:, half_width:])
    far_cols = jnp.where(is_lower, far_white, white)
    far_terms = correlate(far_rows, far_cols, table)

    def trace_valid(valid):
        return jnp.repeat(valid.reshape(-1).astype(jnp.float32), comp_count)

    own_valid = trace_valid(valid_wire)
    near_pairs = jnp.stack(
        [
            (own_valid[:, None] * trace_valid(panels[round_index][1])[None, :]).reshape(-1)
            for round_index in range(near_rounds)
        ],
        0,
    )
    far_trace_valid = trace_valid(far_valid)
    far_row_valid = jnp.where(is_lower, own_valid[:half_width], far_trace_valid[half_width:])
    far_col_valid = jnp.where(is_lower, far_trace_valid, own_valid)
    far_pairs = (far_row_valid[:, None] * far_col_valid[None, :]).reshape(-1)

    hour_devices = math.prod(HOUR_SPLIT)
    share_near = trace_count * trace_count // hour_devices
    share_far = half_width * trace_count // hour_devices
    lag_count = table.shape[1]
    near_slots = near_terms.reshape(near_rounds, hour_devices, share_near, lag_count).transpose(1, 0, 2, 3)
    far_slots = far_terms.reshape(hour_devices, share_far, lag_count)
    count_slots = jnp.concatenate(
        [
            near_pairs.reshape(near_rounds, hour_devices, share_near).transpose(1, 0, 2).reshape(hour_devices, -1),
            far_pairs.reshape(hour_devices, share_far),
        ],
        1,
    )
    row_count = near_rounds * share_near + share_far
    count_row = jnp.pad(count_slots, ((0, 0), (0, lag_count - row_count)))[:, None, :]
    outgoing = jnp.concatenate(
        [near_slots.reshape(hour_devices, near_rounds * share_near, lag_count), far_slots, count_row], 1
    )
    total = outgoing.reshape(HOUR_SPLIT + outgoing.shape[1:])
    for axes, dim in REDUCE_STAGES:
        merged = total.shape[: dim] + (-1,) + total.shape[dim + len(axes) :]
        total = total.reshape(merged)
        total = jnp.sum(lax.all_to_all(total, axes, dim, dim, tiled=True), axis=dim)
    pair_counts = jnp.maximum(total[row_count, :row_count], 1.0)
    stacked = total[:row_count] / pair_counts[:, None]
    near_stack = stacked[: near_rounds * share_near].reshape(near_rounds, share_near, lag_count)
    far_stack = stacked[near_rounds * share_near :]
    return (near_stack[None], far_stack[None])


def solution(mesh):
    hour_mesh = Mesh(
        mesh.devices.reshape(HOUR_SPLIT + (mesh.shape["blocks"],)), HOUR_AXES + ("blocks",)
    )
    in_specs = (P(HOUR_AXES, "blocks", None, None, None), P(HOUR_AXES, "blocks"))
    out_specs = (P("blocks", None, HOUR_AXES, None), P("blocks", HOUR_AXES, None))
    return jax.shard_map(
        on_device, mesh=hour_mesh, in_specs=in_specs, out_specs=out_specs, check_vma=False
    )
```

```python
import math

import jax
import jax.numpy as jnp
from jax import lax
from jax.experimental import pallas as pl
from jax.experimental.pallas import tpu as pltpu
from jax.sharding import Mesh, PartitionSpec as P

BAND = 128
LAGS = 256


EPSILON = 1e-06


HOUR_AXES = ("z_hi", "x", "y", "core")
HOUR_SPLIT = (2, 4, 4, 2)
STACK_STEPS = 8
REDUCE_STAGES = ((("core",), 3), (("x", "y"), 1), (("z_hi",), 0))


def passed_along(block, axis, distance):
    devices = range(lax.axis_size(axis))
    route = [((i - distance) % len(devices), i) for i in devices]
    return lax.ppermute(block, axis, route)


def whiten(spectra, validity, band_width):
    hour_count, station_count, comp_count, part_count, freq_count = spectra.shape
    grouped = spectra.reshape(
        hour_count, station_count, comp_count, part_count, freq_count // band_width, band_width
    )
    band_power = jnp.mean(grouped * grouped, axis=(3, 5), keepdims=True)
    valid_f = validity.astype(jnp.float32).reshape(hour_count, station_count, 1, 1, 1, 1)
    scaled = grouped * (valid_f / jnp.sqrt(band_power + EPSILON))
    return scaled.reshape(hour_count, station_count * comp_count, part_count, freq_count).astype(
        jnp.bfloat16
    )


def build_table(freq_count, lag_count):
    freq_index = jnp.arange(freq_count, dtype=jnp.int32)[:, None]
    lag_index = jnp.arange(lag_count, dtype=jnp.int32)[None, :] - lag_count // 2
    residue = freq_index * (lag_index + 2 * freq_count) % (2 * freq_count)
    angles = residue.astype(jnp.float32) * (math.pi / freq_count)
    amplitude = 8.0 / math.sqrt(freq_count)
    return jnp.concatenate([jnp.cos(angles) * amplitude, -jnp.sin(angles) * amplitude], 0).astype(
        jnp.bfloat16
    )


def cross_spectrum(row_block, col_block):
    row_real = row_block[..., :, None, 0, :].astype(jnp.float32)
    row_imag = row_block[..., :, None, 1, :].astype(jnp.float32)
    col_real = col_block[..., None, :, 0, :].astype(jnp.float32)
    col_imag = col_block[..., None, :, 1, :].astype(jnp.float32)
    real_part = row_real * col_real + row_imag * col_imag
    imag_part = row_imag * col_real - row_real * col_imag
    stacked_parts = jnp.stack([real_part, imag_part], -2)
    dims_shape = stacked_parts.shape
    return stacked_parts.reshape(
        dims_shape[:-4] + (dims_shape[-4] * dims_shape[-3], dims_shape[-2] * dims_shape[-1])
    ).astype(jnp.bfloat16)


def expand(counts, comp_count):
    return jnp.repeat(jnp.repeat(counts, comp_count, 0), comp_count, 1).reshape(-1)


def cross_into(rows_ref, cols_ref, cross_ref):
    row_step = rows_ref.shape[1]
    col_count, wide = cols_ref.shape
    freq_count = wide // 2
    chunk = 256
    for start in range(0, freq_count, chunk):
        col_real = cols_ref[:, start : start + chunk].astype(jnp.float32)
        col_imag = cols_ref[:, freq_count + start : freq_count + start + chunk].astype(jnp.float32)
        for row in range(row_step):
            row_real = rows_ref[0, row : row + 1, start : start + chunk].astype(jnp.float32)
            row_imag = rows_ref[0, row : row + 1, freq_count + start : freq_count + start + chunk]
            row_imag = row_imag.astype(jnp.float32)
            real_part = row_real * col_real + row_imag * col_imag
            imag_part = row_imag * col_real - row_real * col_imag
            first = row * col_count
            cross_ref[first : first + col_count, start : start + chunk] = real_part.astype(jnp.bfloat16)
            cross_ref[first : first + col_count, freq_count + start : freq_count + start + chunk] = (
                imag_part.astype(jnp.bfloat16)
            )


def stack_kernel(
    near_rows_ref, own_ref, passed_ref, far_rows_ref, far_cols_ref, table_ref, count_ref,
    out_ref, near_cross_ref, far_cross_ref,
):
    slots = out_ref.shape[0]
    near_share = near_rows_ref.shape[1] * own_ref.shape[0] // slots
    far_share = far_rows_ref.shape[1] * far_cols_ref.shape[0] // slots
    offset = 0
    for cols_ref in (own_ref, passed_ref):
        cross_into(near_rows_ref, cols_ref, near_cross_ref)
        result = jnp.dot(near_cross_ref[...], table_ref[...], preferred_element_type=jnp.float32)
        for slot in range(slots):
            out_ref[slot, offset : offset + near_share, :] = result[
                slot * near_share : (slot + 1) * near_share
            ]
        offset += near_share
    cross_into(far_rows_ref, far_cols_ref, far_cross_ref)
    result = jnp.dot(far_cross_ref[...], table_ref[...], preferred_element_type=jnp.float32)
    for slot in range(slots):
        out_ref[slot, offset : offset + far_share, :] = result[slot * far_share : (slot + 1) * far_share]
    offset += far_share
    out_ref[:, offset:, :] = count_ref[...]


def stacked_slots(white, passed, far_rows, far_cols, table, count_tail, hour_devices, row_total):
    trace_count, wide = white.shape
    half_width = far_rows.shape[0]
    lag_count = table.shape[1]
    steps = STACK_STEPS
    slots = hour_devices // steps
    near_step = trace_count // steps
    far_step = half_width // steps
    tail = row_total - count_tail.shape[1]
    full = lambda i: (0, 0)
    return pl.pallas_call(
        stack_kernel,
        grid=(steps,),
        in_specs=[
            pl.BlockSpec((1, near_step, wide), lambda i: (i, 0, 0)),
            pl.BlockSpec((trace_count, wide), full),
            pl.BlockSpec((trace_count, wide), full),
            pl.BlockSpec((1, far_step, wide), lambda i: (i, 0, 0)),
            pl.BlockSpec((trace_count, wide), full),
            pl.BlockSpec((wide, lag_count), full),
            pl.BlockSpec((slots, row_total - tail, lag_count), lambda i: (i, 0, 0)),
        ],
        out_specs=pl.BlockSpec((slots, row_total, lag_count), lambda i: (i, 0, 0)),
        out_shape=jax.ShapeDtypeStruct((hour_devices, row_total, lag_count), jnp.float32),
        scratch_shapes=[
            pltpu.VMEM((near_step * trace_count, wide), jnp.bfloat16),
            pltpu.VMEM((far_step * trace_count, wide), jnp.bfloat16),
        ],
    )(
        white.reshape(steps, near_step, wide), white, passed,
        far_rows.reshape(steps, far_step, wide), far_cols, table, count_tail,
    )


def on_device(spectra, validity):
    hour_count, station_count, comp_count, part_count, freq_count = spectra.shape
    trace_count = station_count * comp_count
    half_width = trace_count // 2
    wide = part_count * freq_count
    white = whiten(spectra, validity, BAND).reshape(trace_count, wide)
    table = build_table(freq_count, LAGS)
    valid_wire = validity.astype(jnp.bfloat16)
    block_count = lax.axis_size("blocks")
    near_rounds = block_count // 2
    my_block = lax.axis_index("blocks")
    is_lower = my_block < near_rounds
    panels = [(white, valid_wire)]
    for round_index in range(1, near_rounds + 1):
        panels.append(passed_along((white, valid_wire), "blocks", round_index))
    far_white, far_valid = panels[near_rounds]
    far_rows = jnp.where(is_lower, white[:half_width], far_white[half_width:])
    far_cols = jnp.where(is_lower, far_white, white)

    def trace_valid(valid):
        return jnp.repeat(valid.reshape(-1).astype(jnp.float32), comp_count)

    own_valid = trace_valid(valid_wire)
    near_pairs = jnp.stack(
        [
            (own_valid[:, None] * trace_valid(panels[round_index][1])[None, :]).reshape(-1)
            for round_index in range(near_rounds)
        ],
        0,
    )
    far_trace_valid = trace_valid(far_valid)
    far_row_valid = jnp.where(is_lower, own_valid[:half_width], far_trace_valid[half_width:])
    far_col_valid = jnp.where(is_lower, far_trace_valid, own_valid)
    far_pairs = (far_row_valid[:, None] * far_col_valid[None, :]).reshape(-1)

    hour_devices = math.prod(HOUR_SPLIT)
    share_near = trace_count * trace_count // hour_devices
    share_far = half_width * trace_count // hour_devices
    lag_count = table.shape[1]
    count_slots = jnp.concatenate(
        [
            near_pairs.reshape(near_rounds, hour_devices, share_near).transpose(1, 0, 2).reshape(hour_devices, -1),
            far_pairs.reshape(hour_devices, share_far),
        ],
        1,
    )
    row_count = near_rounds * share_near + share_far
    row_total = -(-(row_count + 1) // 8) * 8
    count_tail = jnp.zeros((hour_devices, row_total - row_count, lag_count), jnp.float32)
    count_tail = count_tail.at[:, 0, :row_count].set(count_slots)
    outgoing = stacked_slots(
        white, panels[1][0], far_rows, far_cols, table, count_tail, hour_devices, row_total
    )
    total = outgoing.reshape(HOUR_SPLIT + outgoing.shape[1:])
    for axes, dim in REDUCE_STAGES:
        merged = total.shape[: dim] + (-1,) + total.shape[dim + len(axes) :]
        total = total.reshape(merged)
        total = jnp.sum(lax.all_to_all(total, axes, dim, dim, tiled=True), axis=dim)
    pair_counts = jnp.maximum(total[row_count, :row_count], 1.0)
    stacked = total[:row_count] / pair_counts[:, None]
    near_stack = stacked[: near_rounds * share_near].reshape(near_rounds, share_near, lag_count)
    far_stack = stacked[near_rounds * share_near :]
    return (near_stack[None], far_stack[None])


def solution(mesh):
    hour_mesh = Mesh(
        mesh.devices.reshape(HOUR_SPLIT + (mesh.shape["blocks"],)), HOUR_AXES + ("blocks",)
    )
    in_specs = (P(HOUR_AXES, "blocks", None, None, None), P(HOUR_AXES, "blocks"))
    out_specs = (P("blocks", None, HOUR_AXES, None), P("blocks", HOUR_AXES, None))
    return jax.shard_map(
        on_device, mesh=hour_mesh, in_specs=in_specs, out_specs=out_specs, check_vma=False
    )
```

```python
import math

import jax
import jax.numpy as jnp
from jax import lax
from jax.experimental import pallas as pl
from jax.experimental.pallas import tpu as pltpu
from jax.sharding import Mesh, PartitionSpec as P

BAND = 128
LAGS = 256


EPSILON = 1e-06


HOUR_AXES = ("z_hi", "x", "y", "core")
HOUR_SPLIT = (2, 4, 4, 2)
STACK_STEPS = 8
REDUCE_STAGES = (
    (("core",), 3, jnp.float32),
    (("x", "y"), 1, jnp.bfloat16),
    (("z_hi",), 0, jnp.float32),
)


def passed_along(block, axis, distance):
    devices = range(lax.axis_size(axis))
    route = [((i - distance) % len(devices), i) for i in devices]
    return lax.ppermute(block, axis, route)


def whiten(spectra, validity, band_width):
    hour_count, station_count, comp_count, part_count, freq_count = spectra.shape
    grouped = spectra.reshape(
        hour_count, station_count, comp_count, part_count, freq_count // band_width, band_width
    )
    band_power = jnp.mean(grouped * grouped, axis=(3, 5), keepdims=True)
    valid_f = validity.astype(jnp.float32).reshape(hour_count, station_count, 1, 1, 1, 1)
    scaled = grouped * (valid_f / jnp.sqrt(band_power + EPSILON))
    return scaled.reshape(hour_count, station_count * comp_count, part_count, freq_count).astype(
        jnp.bfloat16
    )


def build_table(freq_count, lag_count):
    fine_count = 64
    coarse_count = freq_count // fine_count
    lag_index = jnp.arange(lag_count, dtype=jnp.int32)[None, :] - lag_count // 2
    period = 2 * freq_count

    def angle_of(freq_index):
        residue = freq_index[:, None] * (lag_index + period) % period
        return residue.astype(jnp.float32) * (math.pi / freq_count)

    coarse = angle_of(jnp.arange(coarse_count, dtype=jnp.int32) * fine_count)[:, None, :]
    fine = angle_of(jnp.arange(fine_count, dtype=jnp.int32))[None, :, :]
    coarse_cos, coarse_sin = jnp.cos(coarse), jnp.sin(coarse)
    fine_cos, fine_sin = jnp.cos(fine), jnp.sin(fine)
    cos_part = (coarse_cos * fine_cos - coarse_sin * fine_sin).reshape(freq_count, lag_count)
    sin_part = (coarse_sin * fine_cos + coarse_cos * fine_sin).reshape(freq_count, lag_count)
    amplitude = 8.0 / math.sqrt(freq_count)
    return jnp.concatenate([cos_part * amplitude, -sin_part * amplitude], 0).astype(jnp.bfloat16)


def cross_spectrum(row_block, col_block):
    row_real = row_block[..., :, None, 0, :].astype(jnp.float32)
    row_imag = row_block[..., :, None, 1, :].astype(jnp.float32)
    col_real = col_block[..., None, :, 0, :].astype(jnp.float32)
    col_imag = col_block[..., None, :, 1, :].astype(jnp.float32)
    real_part = row_real * col_real + row_imag * col_imag
    imag_part = row_imag * col_real - row_real * col_imag
    stacked_parts = jnp.stack([real_part, imag_part], -2)
    dims_shape = stacked_parts.shape
    return stacked_parts.reshape(
        dims_shape[:-4] + (dims_shape[-4] * dims_shape[-3], dims_shape[-2] * dims_shape[-1])
    ).astype(jnp.bfloat16)


def expand(counts, comp_count):
    return jnp.repeat(jnp.repeat(counts, comp_count, 0), comp_count, 1).reshape(-1)


def cross_into(rows_ref, cols_ref, cross_ref):
    row_step = rows_ref.shape[1]
    col_count, wide = cols_ref.shape
    freq_count = wide // 2
    chunk = 256
    for start in range(0, freq_count, chunk):
        col_real = cols_ref[:, start : start + chunk].astype(jnp.float32)
        col_imag = cols_ref[:, freq_count + start : freq_count + start + chunk].astype(jnp.float32)
        for row in range(row_step):
            row_real = rows_ref[0, row : row + 1, start : start + chunk].astype(jnp.float32)
            row_imag = rows_ref[0, row : row + 1, freq_count + start : freq_count + start + chunk]
            row_imag = row_imag.astype(jnp.float32)
            real_part = row_real * col_real + row_imag * col_imag
            imag_part = row_imag * col_real - row_real * col_imag
            first = row * col_count
            cross_ref[first : first + col_count, start : start + chunk] = real_part.astype(jnp.bfloat16)
            cross_ref[first : first + col_count, freq_count + start : freq_count + start + chunk] = (
                imag_part.astype(jnp.bfloat16)
            )


def stack_kernel(
    near_rows_ref, own_ref, passed_ref, far_rows_ref, far_cols_ref, table_ref, count_ref,
    out_ref, near_cross_ref, far_cross_ref,
):
    slots = out_ref.shape[0]
    near_share = near_rows_ref.shape[1] * own_ref.shape[0] // slots
    far_share = far_rows_ref.shape[1] * far_cols_ref.shape[0] // slots
    offset = 0
    for cols_ref in (own_ref, passed_ref):
        cross_into(near_rows_ref, cols_ref, near_cross_ref)
        result = jnp.dot(near_cross_ref[...], table_ref[...], preferred_element_type=jnp.float32)
        for slot in range(slots):
            out_ref[slot, offset : offset + near_share, :] = result[
                slot * near_share : (slot + 1) * near_share
            ]
        offset += near_share
    cross_into(far_rows_ref, far_cols_ref, far_cross_ref)
    result = jnp.dot(far_cross_ref[...], table_ref[...], preferred_element_type=jnp.float32)
    for slot in range(slots):
        out_ref[slot, offset : offset + far_share, :] = result[slot * far_share : (slot + 1) * far_share]
    offset += far_share
    out_ref[:, offset:, :] = count_ref[...]


def stacked_slots(white, passed, far_rows, far_cols, table, count_tail, hour_devices, row_total):
    trace_count, wide = white.shape
    half_width = far_rows.shape[0]
    lag_count = table.shape[1]
    steps = STACK_STEPS
    slots = hour_devices // steps
    near_step = trace_count // steps
    far_step = half_width // steps
    tail = row_total - count_tail.shape[1]
    full = lambda i: (0, 0)
    return pl.pallas_call(
        stack_kernel,
        grid=(steps,),
        in_specs=[
            pl.BlockSpec((1, near_step, wide), lambda i: (i, 0, 0)),
            pl.BlockSpec((trace_count, wide), full),
            pl.BlockSpec((trace_count, wide), full),
            pl.BlockSpec((1, far_step, wide), lambda i: (i, 0, 0)),
            pl.BlockSpec((trace_count, wide), full),
            pl.BlockSpec((wide, lag_count), full),
            pl.BlockSpec((slots, row_total - tail, lag_count), lambda i: (i, 0, 0)),
        ],
        out_specs=pl.BlockSpec((slots, row_total, lag_count), lambda i: (i, 0, 0)),
        out_shape=jax.ShapeDtypeStruct((hour_devices, row_total, lag_count), jnp.float32),
        scratch_shapes=[
            pltpu.VMEM((near_step * trace_count, wide), jnp.bfloat16),
            pltpu.VMEM((far_step * trace_count, wide), jnp.bfloat16),
        ],
    )(
        white.reshape(steps, near_step, wide), white, passed,
        far_rows.reshape(steps, far_step, wide), far_cols, table, count_tail,
    )


def on_device(spectra, validity):
    hour_count, station_count, comp_count, part_count, freq_count = spectra.shape
    trace_count = station_count * comp_count
    half_width = trace_count // 2
    wide = part_count * freq_count
    white = whiten(spectra, validity, BAND).reshape(trace_count, wide)
    table = build_table(freq_count, LAGS)
    valid_wire = validity.astype(jnp.bfloat16)
    block_count = lax.axis_size("blocks")
    near_rounds = block_count // 2
    my_block = lax.axis_index("blocks")
    is_lower = my_block < near_rounds
    panels = [(white, valid_wire)]
    for round_index in range(1, near_rounds + 1):
        panels.append(passed_along((white, valid_wire), "blocks", round_index))
    far_white, far_valid = panels[near_rounds]
    far_rows = jnp.where(is_lower, white[:half_width], far_white[half_width:])
    far_cols = jnp.where(is_lower, far_white, white)

    def trace_valid(valid):
        return jnp.repeat(valid.reshape(-1).astype(jnp.float32), comp_count)

    own_valid = trace_valid(valid_wire)
    near_pairs = jnp.stack(
        [
            (own_valid[:, None] * trace_valid(panels[round_index][1])[None, :]).reshape(-1)
            for round_index in range(near_rounds)
        ],
        0,
    )
    far_trace_valid = trace_valid(far_valid)
    far_row_valid = jnp.where(is_lower, own_valid[:half_width], far_trace_valid[half_width:])
    far_col_valid = jnp.where(is_lower, far_trace_valid, own_valid)
    far_pairs = (far_row_valid[:, None] * far_col_valid[None, :]).reshape(-1)

    hour_devices = math.prod(HOUR_SPLIT)
    share_near = trace_count * trace_count // hour_devices
    share_far = half_width * trace_count // hour_devices
    lag_count = table.shape[1]
    count_slots = jnp.concatenate(
        [
            near_pairs.reshape(near_rounds, hour_devices, share_near).transpose(1, 0, 2).reshape(hour_devices, -1),
            far_pairs.reshape(hour_devices, share_far),
        ],
        1,
    )
    row_count = near_rounds * share_near + share_far
    row_total = -(-(row_count + 1) // 8) * 8
    count_tail = jnp.zeros((hour_devices, row_total - row_count, lag_count), jnp.float32)
    count_tail = count_tail.at[:, 0, :row_count].set(count_slots)
    outgoing = stacked_slots(
        white, panels[1][0], far_rows, far_cols, table, count_tail, hour_devices, row_total
    )
    total = outgoing.reshape(HOUR_SPLIT + outgoing.shape[1:])
    for axes, dim, wire in REDUCE_STAGES:
        merged = total.shape[: dim] + (-1,) + total.shape[dim + len(axes) :]
        total = total.reshape(merged).astype(wire)
        incoming = lax.all_to_all(total, axes, dim, dim, tiled=True)
        total = jnp.sum(incoming.astype(jnp.float32), axis=dim)
    pair_counts = jnp.maximum(total[row_count, :row_count], 1.0)
    stacked = total[:row_count] / pair_counts[:, None]
    near_stack = stacked[: near_rounds * share_near].reshape(near_rounds, share_near, lag_count)
    far_stack = stacked[near_rounds * share_near :]
    return (near_stack[None], far_stack[None])


def solution(mesh):
    hour_mesh = Mesh(
        mesh.devices.reshape(HOUR_SPLIT + (mesh.shape["blocks"],)), HOUR_AXES + ("blocks",)
    )
    in_specs = (P(HOUR_AXES, "blocks", None, None, None), P(HOUR_AXES, "blocks"))
    out_specs = (P("blocks", None, HOUR_AXES, None), P("blocks", HOUR_AXES, None))
    return jax.shard_map(
        on_device, mesh=hour_mesh, in_specs=in_specs, out_specs=out_specs, check_vma=False
    )
```

```python
import math

import jax
import jax.numpy as jnp
from jax import lax
from jax.experimental import pallas as pl
from jax.experimental.pallas import tpu as pltpu
from jax.sharding import Mesh, PartitionSpec as P

BAND = 128
LAGS = 256


EPSILON = 1e-06


HOUR_AXES = ("z_hi", "x", "y", "core")
HOUR_SPLIT = (2, 4, 4, 2)
STACK_STEPS = 8


def passed_along(block, axis, distance):
    devices = range(lax.axis_size(axis))
    route = [((i - distance) % len(devices), i) for i in devices]
    return lax.ppermute(block, axis, route)


def whiten(spectra, validity, band_width):
    hour_count, station_count, comp_count, part_count, freq_count = spectra.shape
    grouped = spectra.reshape(
        hour_count, station_count, comp_count, part_count, freq_count // band_width, band_width
    )
    band_power = jnp.mean(grouped * grouped, axis=(3, 5), keepdims=True)
    valid_f = validity.astype(jnp.float32).reshape(hour_count, station_count, 1, 1, 1, 1)
    scaled = grouped * (valid_f / jnp.sqrt(band_power + EPSILON))
    return scaled.reshape(hour_count, station_count * comp_count, part_count, freq_count).astype(
        jnp.bfloat16
    )


def build_table(freq_count, lag_count):
    fine_count = 64
    coarse_count = freq_count // fine_count
    lag_index = jnp.arange(lag_count, dtype=jnp.int32)[None, :] - lag_count // 2
    period = 2 * freq_count

    def angle_of(freq_index):
        residue = freq_index[:, None] * (lag_index + period) % period
        return residue.astype(jnp.float32) * (math.pi / freq_count)

    coarse = angle_of(jnp.arange(coarse_count, dtype=jnp.int32) * fine_count)[:, None, :]
    fine = angle_of(jnp.arange(fine_count, dtype=jnp.int32))[None, :, :]
    coarse_cos, coarse_sin = jnp.cos(coarse), jnp.sin(coarse)
    fine_cos, fine_sin = jnp.cos(fine), jnp.sin(fine)
    cos_part = (coarse_cos * fine_cos - coarse_sin * fine_sin).reshape(freq_count, lag_count)
    sin_part = (coarse_sin * fine_cos + coarse_cos * fine_sin).reshape(freq_count, lag_count)
    amplitude = 8.0 / math.sqrt(freq_count)
    return jnp.concatenate([cos_part * amplitude, -sin_part * amplitude], 0).astype(jnp.bfloat16)


def cross_spectrum(row_block, col_block):
    row_real = row_block[..., :, None, 0, :].astype(jnp.float32)
    row_imag = row_block[..., :, None, 1, :].astype(jnp.float32)
    col_real = col_block[..., None, :, 0, :].astype(jnp.float32)
    col_imag = col_block[..., None, :, 1, :].astype(jnp.float32)
    real_part = row_real * col_real + row_imag * col_imag
    imag_part = row_imag * col_real - row_real * col_imag
    stacked_parts = jnp.stack([real_part, imag_part], -2)
    dims_shape = stacked_parts.shape
    return stacked_parts.reshape(
        dims_shape[:-4] + (dims_shape[-4] * dims_shape[-3], dims_shape[-2] * dims_shape[-1])
    ).astype(jnp.bfloat16)


def expand(counts, comp_count):
    return jnp.repeat(jnp.repeat(counts, comp_count, 0), comp_count, 1).reshape(-1)


def cross_into(rows_ref, cols_ref, cross_ref):
    row_step = rows_ref.shape[1]
    col_count, wide = cols_ref.shape
    freq_count = wide // 2
    chunk = 256
    for start in range(0, freq_count, chunk):
        col_real = cols_ref[:, start : start + chunk].astype(jnp.float32)
        col_imag = cols_ref[:, freq_count + start : freq_count + start + chunk].astype(jnp.float32)
        for row in range(row_step):
            row_real = rows_ref[0, row : row + 1, start : start + chunk].astype(jnp.float32)
            row_imag = rows_ref[0, row : row + 1, freq_count + start : freq_count + start + chunk]
            row_imag = row_imag.astype(jnp.float32)
            real_part = row_real * col_real + row_imag * col_imag
            imag_part = row_imag * col_real - row_real * col_imag
            first = row * col_count
            cross_ref[first : first + col_count, start : start + chunk] = real_part.astype(jnp.bfloat16)
            cross_ref[first : first + col_count, freq_count + start : freq_count + start + chunk] = (
                imag_part.astype(jnp.bfloat16)
            )


def stack_kernel(
    near_rows_ref, own_ref, passed_ref, far_rows_ref, far_cols_ref, table_ref, count_ref,
    out_ref, near_cross_ref, far_cross_ref,
):
    minor, major = out_ref.shape[:2]
    slots = minor * major
    near_share = near_rows_ref.shape[1] * own_ref.shape[0] // slots
    far_share = far_rows_ref.shape[1] * far_cols_ref.shape[0] // slots
    offset = 0
    for cols_ref in (own_ref, passed_ref):
        cross_into(near_rows_ref, cols_ref, near_cross_ref)
        result = jnp.dot(near_cross_ref[...], table_ref[...], preferred_element_type=jnp.float32)
        for slot in range(slots):
            out_ref[slot % minor, slot // minor, offset : offset + near_share, :] = result[
                slot * near_share : (slot + 1) * near_share
            ]
        offset += near_share
    cross_into(far_rows_ref, far_cols_ref, far_cross_ref)
    result = jnp.dot(far_cross_ref[...], table_ref[...], preferred_element_type=jnp.float32)
    for slot in range(slots):
        out_ref[slot % minor, slot // minor, offset : offset + far_share, :] = result[
            slot * far_share : (slot + 1) * far_share
        ]
    offset += far_share
    out_ref[:, :, offset:, :] = count_ref[...]


def stacked_slots(white, passed, far_rows, far_cols, table, count_tail, hour_devices, row_total):
    trace_count, wide = white.shape
    half_width = far_rows.shape[0]
    lag_count = table.shape[1]
    steps = STACK_STEPS
    slots = hour_devices // steps
    minor = HOUR_SPLIT[-1]
    near_step = trace_count // steps
    far_step = half_width // steps
    tail = row_total - count_tail.shape[2]
    full = lambda i: (0, 0)
    return pl.pallas_call(
        stack_kernel,
        grid=(steps,),
        in_specs=[
            pl.BlockSpec((1, near_step, wide), lambda i: (i, 0, 0)),
            pl.BlockSpec((trace_count, wide), full),
            pl.BlockSpec((trace_count, wide), full),
            pl.BlockSpec((1, far_step, wide), lambda i: (i, 0, 0)),
            pl.BlockSpec((trace_count, wide), full),
            pl.BlockSpec((wide, lag_count), full),
            pl.BlockSpec((minor, slots // minor, row_total - tail, lag_count), lambda i: (0, i, 0, 0)),
        ],
        out_specs=pl.BlockSpec((minor, slots // minor, row_total, lag_count), lambda i: (0, i, 0, 0)),
        out_shape=jax.ShapeDtypeStruct(
            (minor, hour_devices // minor, row_total, lag_count), jnp.float32
        ),
        scratch_shapes=[
            pltpu.VMEM((near_step * trace_count, wide), jnp.bfloat16),
            pltpu.VMEM((far_step * trace_count, wide), jnp.bfloat16),
        ],
    )(
        white.reshape(steps, near_step, wide), white, passed,
        far_rows.reshape(steps, far_step, wide), far_cols, table, count_tail,
    )


def on_device(spectra, validity):
    hour_count, station_count, comp_count, part_count, freq_count = spectra.shape
    trace_count = station_count * comp_count
    half_width = trace_count // 2
    wide = part_count * freq_count
    white = whiten(spectra, validity, BAND).reshape(trace_count, wide)
    table = build_table(freq_count, LAGS)
    valid_wire = validity.astype(jnp.bfloat16)
    block_count = lax.axis_size("blocks")
    near_rounds = block_count // 2
    my_block = lax.axis_index("blocks")
    is_lower = my_block < near_rounds
    panels = [(white, valid_wire)]
    for round_index in range(1, near_rounds + 1):
        panels.append(passed_along((white, valid_wire), "blocks", round_index))
    far_white, far_valid = panels[near_rounds]
    far_rows = jnp.where(is_lower, white[:half_width], far_white[half_width:])
    far_cols = jnp.where(is_lower, far_white, white)

    def trace_valid(valid):
        return jnp.repeat(valid.reshape(-1).astype(jnp.float32), comp_count)

    own_valid = trace_valid(valid_wire)
    near_pairs = jnp.stack(
        [
            (own_valid[:, None] * trace_valid(panels[round_index][1])[None, :]).reshape(-1)
            for round_index in range(near_rounds)
        ],
        0,
    )
    far_trace_valid = trace_valid(far_valid)
    far_row_valid = jnp.where(is_lower, own_valid[:half_width], far_trace_valid[half_width:])
    far_col_valid = jnp.where(is_lower, far_trace_valid, own_valid)
    far_pairs = (far_row_valid[:, None] * far_col_valid[None, :]).reshape(-1)

    hour_devices = math.prod(HOUR_SPLIT)
    share_near = trace_count * trace_count // hour_devices
    share_far = half_width * trace_count // hour_devices
    lag_count = table.shape[1]
    count_slots = jnp.concatenate(
        [
            near_pairs.reshape(near_rounds, hour_devices, share_near).transpose(1, 0, 2).reshape(hour_devices, -1),
            far_pairs.reshape(hour_devices, share_far),
        ],
        1,
    )
    row_count = near_rounds * share_near + share_far
    row_total = -(-(row_count + 1) // 8) * 8
    count_tail = jnp.zeros((hour_devices, row_total - row_count, lag_count), jnp.float32)
    count_tail = count_tail.at[:, 0, :row_count].set(count_slots)
    minor = HOUR_SPLIT[-1]
    count_tail = count_tail.reshape((hour_devices // minor, minor) + count_tail.shape[1:])
    count_tail = count_tail.transpose(1, 0, 2, 3)
    outgoing = stacked_slots(
        white, panels[1][0], far_rows, far_cols, table, count_tail, hour_devices, row_total
    )
    total = jnp.sum(lax.all_to_all(outgoing, "core", 0, 0, tiled=True), axis=0)
    total = total.reshape((HOUR_SPLIT[0], -1) + total.shape[1:]).astype(jnp.bfloat16)
    incoming = lax.all_to_all(total, ("x", "y"), 1, 1, tiled=True)
    total = jnp.sum(incoming.astype(jnp.float32), axis=1)
    upper = lax.axis_index("z_hi") > 0
    kept = jnp.where(upper, total[1], total[0])
    sent = jnp.where(upper, total[0], total[1])
    total = kept + lax.ppermute(sent, "z_hi", [(0, 1), (1, 0)])
    pair_counts = jnp.maximum(total[row_count, :row_count], 1.0)
    stacked = total[:row_count] / pair_counts[:, None]
    near_stack = stacked[: near_rounds * share_near].reshape(near_rounds, share_near, lag_count)
    far_stack = stacked[near_rounds * share_near :]
    return (near_stack[None], far_stack[None])


def solution(mesh):
    hour_mesh = Mesh(
        mesh.devices.reshape(HOUR_SPLIT + (mesh.shape["blocks"],)), HOUR_AXES + ("blocks",)
    )
    in_specs = (P(HOUR_AXES, "blocks", None, None, None), P(HOUR_AXES, "blocks"))
    out_specs = (P("blocks", None, HOUR_AXES, None), P("blocks", HOUR_AXES, None))
    return jax.shard_map(
        on_device, mesh=hour_mesh, in_specs=in_specs, out_specs=out_specs, check_vma=False
    )
```

```python
import math

import jax
import jax.numpy as jnp
from jax import lax
from jax.experimental import pallas as pl
from jax.experimental.pallas import tpu as pltpu
from jax.sharding import Mesh, PartitionSpec as P

BAND = 128
LAGS = 256


EPSILON = 1e-06


HOUR_AXES = ("z_hi", "x", "y", "core")
HOUR_SPLIT = (2, 4, 4, 2)
STACK_STEPS = 8


def passed_along(block, axis, distance):
    devices = range(lax.axis_size(axis))
    route = [((i - distance) % len(devices), i) for i in devices]
    return lax.ppermute(block, axis, route)


def whiten(spectra, validity, band_width):
    hour_count, station_count, comp_count, part_count, freq_count = spectra.shape
    grouped = spectra.reshape(
        hour_count, station_count, comp_count, part_count, freq_count // band_width, band_width
    )
    band_power = jnp.mean(grouped * grouped, axis=(3, 5), keepdims=True)
    valid_f = validity.astype(jnp.float32).reshape(hour_count, station_count, 1, 1, 1, 1)
    scaled = grouped * (valid_f / jnp.sqrt(band_power + EPSILON))
    return scaled.reshape(hour_count, station_count * comp_count, part_count, freq_count).astype(
        jnp.bfloat16
    )


def build_table(freq_count, lag_count):
    fine_count = 64
    coarse_count = freq_count // fine_count
    lag_index = jnp.arange(lag_count, dtype=jnp.int32)[None, :] - lag_count // 2
    period = 2 * freq_count

    def angle_of(freq_index):
        residue = freq_index[:, None] * (lag_index + period) % period
        return residue.astype(jnp.float32) * (math.pi / freq_count)

    coarse = angle_of(jnp.arange(coarse_count, dtype=jnp.int32) * fine_count)[:, None, :]
    fine = angle_of(jnp.arange(fine_count, dtype=jnp.int32))[None, :, :]
    coarse_cos, coarse_sin = jnp.cos(coarse), jnp.sin(coarse)
    fine_cos, fine_sin = jnp.cos(fine), jnp.sin(fine)
    cos_part = (coarse_cos * fine_cos - coarse_sin * fine_sin).reshape(freq_count, lag_count)
    sin_part = (coarse_sin * fine_cos + coarse_cos * fine_sin).reshape(freq_count, lag_count)
    amplitude = 8.0 / math.sqrt(freq_count)
    return jnp.concatenate([cos_part * amplitude, -sin_part * amplitude], 0).astype(jnp.bfloat16)


def cross_spectrum(row_block, col_block):
    row_real = row_block[..., :, None, 0, :].astype(jnp.float32)
    row_imag = row_block[..., :, None, 1, :].astype(jnp.float32)
    col_real = col_block[..., None, :, 0, :].astype(jnp.float32)
    col_imag = col_block[..., None, :, 1, :].astype(jnp.float32)
    real_part = row_real * col_real + row_imag * col_imag
    imag_part = row_imag * col_real - row_real * col_imag
    stacked_parts = jnp.stack([real_part, imag_part], -2)
    dims_shape = stacked_parts.shape
    return stacked_parts.reshape(
        dims_shape[:-4] + (dims_shape[-4] * dims_shape[-3], dims_shape[-2] * dims_shape[-1])
    ).astype(jnp.bfloat16)


def expand(counts, comp_count):
    return jnp.repeat(jnp.repeat(counts, comp_count, 0), comp_count, 1).reshape(-1)


def cross_into(rows_ref, cols_ref, cross_ref):
    row_step = rows_ref.shape[1]
    col_count, wide = cols_ref.shape
    freq_count = wide // 2
    chunk = 256
    for start in range(0, freq_count, chunk):
        col_real = cols_ref[:, start : start + chunk].astype(jnp.float32)
        col_imag = cols_ref[:, freq_count + start : freq_count + start + chunk].astype(jnp.float32)
        for row in range(row_step):
            row_real = rows_ref[0, row : row + 1, start : start + chunk].astype(jnp.float32)
            row_imag = rows_ref[0, row : row + 1, freq_count + start : freq_count + start + chunk]
            row_imag = row_imag.astype(jnp.float32)
            real_part = row_real * col_real + row_imag * col_imag
            imag_part = row_imag * col_real - row_real * col_imag
            first = row * col_count
            cross_ref[first : first + col_count, start : start + chunk] = real_part.astype(jnp.bfloat16)
            cross_ref[first : first + col_count, freq_count + start : freq_count + start + chunk] = (
                imag_part.astype(jnp.bfloat16)
            )


def slot_rows(result, out_ref, offset, share):
    minor, major = out_ref.shape[:2]
    for slot in range(minor * major):
        out_ref[slot % minor, slot // minor, offset : offset + share, :] = result[
            slot * share : (slot + 1) * share
        ]


def correlated(rows_ref, cols_ref, table_ref, cross_ref):
    cross_into(rows_ref, cols_ref, cross_ref)
    return jnp.dot(cross_ref[...], table_ref[...], preferred_element_type=jnp.float32)


def own_kernel(near_rows_ref, own_ref, table_ref, count_ref, out_ref, cross_ref):
    slots = out_ref.shape[0] * out_ref.shape[1]
    near_share = near_rows_ref.shape[1] * own_ref.shape[0] // slots
    slot_rows(correlated(near_rows_ref, own_ref, table_ref, cross_ref), out_ref, 0, near_share)
    out_ref[:, :, out_ref.shape[2] - count_ref.shape[2] :, :] = count_ref[...]


def passed_kernel(
    prev_ref, near_rows_ref, passed_ref, far_rows_ref, far_cols_ref, table_ref,
    out_ref, near_cross_ref, far_cross_ref,
):
    slots = out_ref.shape[0] * out_ref.shape[1]
    near_share = near_rows_ref.shape[1] * passed_ref.shape[0] // slots
    far_share = far_rows_ref.shape[1] * far_cols_ref.shape[0] // slots
    tail_start = 2 * near_share + far_share
    out_ref[:, :, :near_share, :] = prev_ref[:, :, :near_share, :]
    out_ref[:, :, tail_start:, :] = prev_ref[:, :, tail_start:, :]
    result = correlated(near_rows_ref, passed_ref, table_ref, near_cross_ref)
    slot_rows(result, out_ref, near_share, near_share)
    result = correlated(far_rows_ref, far_cols_ref, table_ref, far_cross_ref)
    slot_rows(result, out_ref, 2 * near_share, far_share)


def own_slots(white, table, count_tail, hour_devices, row_total):
    trace_count, wide = white.shape
    lag_count = table.shape[1]
    steps = STACK_STEPS
    slots = hour_devices // steps
    minor = HOUR_SPLIT[-1]
    near_step = trace_count // steps
    tail = count_tail.shape[2]
    full = lambda i: (0, 0)
    return pl.pallas_call(
        own_kernel,
        grid=(steps,),
        in_specs=[
            pl.BlockSpec((1, near_step, wide), lambda i: (i, 0, 0)),
            pl.BlockSpec((trace_count, wide), full),
            pl.BlockSpec((wide, lag_count), full),
            pl.BlockSpec((minor, slots // minor, tail, lag_count), lambda i: (0, i, 0, 0)),
        ],
        out_specs=pl.BlockSpec((minor, slots // minor, row_total, lag_count), lambda i: (0, i, 0, 0)),
        out_shape=jax.ShapeDtypeStruct(
            (minor, hour_devices // minor, row_total, lag_count), jnp.float32
        ),
        scratch_shapes=[pltpu.VMEM((near_step * trace_count, wide), jnp.bfloat16)],
    )(white.reshape(steps, near_step, wide), white, table, count_tail)


def passed_slots(prev, white, passed, far_rows, far_cols, table):
    trace_count, wide = white.shape
    half_width = far_rows.shape[0]
    lag_count = table.shape[1]
    minor, major, row_total = prev.shape[:3]
    steps = STACK_STEPS
    near_step = trace_count // steps
    far_step = half_width // steps
    full = lambda i: (0, 0)
    slot_block = pl.BlockSpec((minor, major // steps, row_total, lag_count), lambda i: (0, i, 0, 0))
    return pl.pallas_call(
        passed_kernel,
        grid=(steps,),
        in_specs=[
            slot_block,
            pl.BlockSpec((1, near_step, wide), lambda i: (i, 0, 0)),
            pl.BlockSpec((trace_count, wide), full),
            pl.BlockSpec((1, far_step, wide), lambda i: (i, 0, 0)),
            pl.BlockSpec((trace_count, wide), full),
            pl.BlockSpec((wide, lag_count), full),
        ],
        out_specs=slot_block,
        out_shape=jax.ShapeDtypeStruct(prev.shape, jnp.float32),
        scratch_shapes=[
            pltpu.VMEM((near_step * trace_count, wide), jnp.bfloat16),
            pltpu.VMEM((far_step * trace_count, wide), jnp.bfloat16),
        ],
        input_output_aliases={0: 0},
    )(prev, white.reshape(steps, near_step, wide), passed, far_rows.reshape(steps, far_step, wide), far_cols, table)


def on_device(spectra, validity):
    hour_count, station_count, comp_count, part_count, freq_count = spectra.shape
    trace_count = station_count * comp_count
    half_width = trace_count // 2
    wide = part_count * freq_count
    white = whiten(spectra, validity, BAND).reshape(trace_count, wide)
    table = build_table(freq_count, LAGS)
    valid_wire = validity.astype(jnp.bfloat16)
    block_count = lax.axis_size("blocks")
    near_rounds = block_count // 2
    my_block = lax.axis_index("blocks")
    is_lower = my_block < near_rounds
    panels = [(white, valid_wire)]
    for round_index in range(1, near_rounds + 1):
        panels.append(passed_along((white, valid_wire), "blocks", round_index))
    far_white, far_valid = panels[near_rounds]
    far_rows = jnp.where(is_lower, white[:half_width], far_white[half_width:])
    far_cols = jnp.where(is_lower, far_white, white)

    def trace_valid(valid):
        return jnp.repeat(valid.reshape(-1).astype(jnp.float32), comp_count)

    own_valid = trace_valid(valid_wire)
    near_pairs = jnp.stack(
        [
            (own_valid[:, None] * trace_valid(panels[round_index][1])[None, :]).reshape(-1)
            for round_index in range(near_rounds)
        ],
        0,
    )
    far_trace_valid = trace_valid(far_valid)
    far_row_valid = jnp.where(is_lower, own_valid[:half_width], far_trace_valid[half_width:])
    far_col_valid = jnp.where(is_lower, far_trace_valid, own_valid)
    far_pairs = (far_row_valid[:, None] * far_col_valid[None, :]).reshape(-1)

    hour_devices = math.prod(HOUR_SPLIT)
    share_near = trace_count * trace_count // hour_devices
    share_far = half_width * trace_count // hour_devices
    lag_count = table.shape[1]
    count_slots = jnp.concatenate(
        [
            near_pairs.reshape(near_rounds, hour_devices, share_near).transpose(1, 0, 2).reshape(hour_devices, -1),
            far_pairs.reshape(hour_devices, share_far),
        ],
        1,
    )
    row_count = near_rounds * share_near + share_far
    row_total = -(-(row_count + 1) // 8) * 8
    count_tail = jnp.zeros((hour_devices, row_total - row_count, lag_count), jnp.float32)
    count_tail = count_tail.at[:, 0, :row_count].set(count_slots)
    minor = HOUR_SPLIT[-1]
    count_tail = count_tail.reshape((hour_devices // minor, minor) + count_tail.shape[1:])
    count_tail = count_tail.transpose(1, 0, 2, 3)
    outgoing = own_slots(white, table, count_tail, hour_devices, row_total)
    outgoing = passed_slots(outgoing, white, panels[1][0], far_rows, far_cols, table)
    total = jnp.sum(lax.all_to_all(outgoing, "core", 0, 0, tiled=True), axis=0)
    total = total.reshape((HOUR_SPLIT[0], -1) + total.shape[1:]).astype(jnp.bfloat16)
    incoming = lax.all_to_all(total, ("x", "y"), 1, 1, tiled=True)
    total = jnp.sum(incoming.astype(jnp.float32), axis=1)
    upper = lax.axis_index("z_hi") > 0
    kept = jnp.where(upper, total[1], total[0])
    sent = jnp.where(upper, total[0], total[1])
    total = kept + lax.ppermute(sent, "z_hi", [(0, 1), (1, 0)])
    pair_counts = jnp.maximum(total[row_count, :row_count], 1.0)
    stacked = total[:row_count] / pair_counts[:, None]
    near_stack = stacked[: near_rounds * share_near].reshape(near_rounds, share_near, lag_count)
    far_stack = stacked[near_rounds * share_near :]
    return (near_stack[None], far_stack[None])


def solution(mesh):
    hour_mesh = Mesh(
        mesh.devices.reshape(HOUR_SPLIT + (mesh.shape["blocks"],)), HOUR_AXES + ("blocks",)
    )
    in_specs = (P(HOUR_AXES, "blocks", None, None, None), P(HOUR_AXES, "blocks"))
    out_specs = (P("blocks", None, HOUR_AXES, None), P("blocks", HOUR_AXES, None))
    return jax.shard_map(
        on_device, mesh=hour_mesh, in_specs=in_specs, out_specs=out_specs, check_vma=False
    )
```

```python
import math

import jax
import jax.numpy as jnp
from jax import lax
from jax.experimental import pallas as pl
from jax.experimental.pallas import tpu as pltpu
from jax.sharding import Mesh, PartitionSpec as P


BAND = 128
LAGS = 256


EPSILON = 1e-06


HOUR_AXES = ("z_hi", "x", "y", "core")
HOUR_SPLIT = (2, 4, 4, 2)
STACK_STEPS = 4


def passed_along(block, axis, distance):
    devices = range(lax.axis_size(axis))
    route = [((i - distance) % len(devices), i) for i in devices]
    return lax.ppermute(block, axis, route)


def whiten(spectra, validity, band_width):
    hour_count, station_count, comp_count, part_count, freq_count = spectra.shape
    grouped = spectra.reshape(
        hour_count, station_count, comp_count, part_count, freq_count // band_width, band_width
    )
    band_power = jnp.mean(grouped * grouped, axis=(3, 5), keepdims=True)
    valid_f = validity.astype(jnp.float32).reshape(hour_count, station_count, 1, 1, 1, 1)
    scaled = grouped * (valid_f / jnp.sqrt(band_power + EPSILON))
    return scaled.reshape(hour_count, station_count * comp_count, part_count, freq_count).astype(
        jnp.bfloat16
    )


def build_table(freq_count, lag_count):
    fine_count = 64
    coarse_count = freq_count // fine_count
    lag_index = jnp.arange(lag_count, dtype=jnp.int32)[None, :] - lag_count // 2
    period = 2 * freq_count

    def angle_of(freq_index):
        residue = freq_index[:, None] * (lag_index + period) % period
        return residue.astype(jnp.float32) * (math.pi / freq_count)

    coarse = angle_of(jnp.arange(coarse_count, dtype=jnp.int32) * fine_count)[:, None, :]
    fine = angle_of(jnp.arange(fine_count, dtype=jnp.int32))[None, :, :]
    coarse_cos, coarse_sin = jnp.cos(coarse), jnp.sin(coarse)
    fine_cos, fine_sin = jnp.cos(fine), jnp.sin(fine)
    cos_part = (coarse_cos * fine_cos - coarse_sin * fine_sin).reshape(freq_count, lag_count)
    sin_part = (coarse_sin * fine_cos + coarse_cos * fine_sin).reshape(freq_count, lag_count)
    amplitude = 8.0 / math.sqrt(freq_count)
    return jnp.concatenate([cos_part * amplitude, -sin_part * amplitude], 0).astype(jnp.bfloat16)


def cross_into(rows_ref, cols_ref, cross_ref):
    row_step = rows_ref.shape[1]
    col_count, wide = cols_ref.shape
    freq_count = wide // 2
    chunk = 256
    for start in range(0, freq_count, chunk):
        col_real = cols_ref[:, start : start + chunk].astype(jnp.float32)
        col_imag = cols_ref[:, freq_count + start : freq_count + start + chunk].astype(jnp.float32)
        for row in range(row_step):
            row_real = rows_ref[0, row : row + 1, start : start + chunk].astype(jnp.float32)
            row_imag = rows_ref[0, row : row + 1, freq_count + start : freq_count + start + chunk]
            row_imag = row_imag.astype(jnp.float32)
            real_part = row_real * col_real + row_imag * col_imag
            imag_part = row_imag * col_real - row_real * col_imag
            first = row * col_count
            cross_ref[first : first + col_count, start : start + chunk] = real_part.astype(jnp.bfloat16)
            cross_ref[first : first + col_count, freq_count + start : freq_count + start + chunk] = (
                imag_part.astype(jnp.bfloat16)
            )


def slot_rows(result, out_ref, offset, share):
    minor, major = out_ref.shape[:2]
    for slot in range(minor * major):
        out_ref[slot % minor, slot // minor, offset : offset + share, :] = result[
            slot * share : (slot + 1) * share
        ]


def correlated(rows_ref, cols_ref, table_ref, cross_ref):
    cross_into(rows_ref, cols_ref, cross_ref)
    return jnp.dot(cross_ref[...], table_ref[...], preferred_element_type=jnp.float32)


def own_kernel(near_rows_ref, own_ref, table_ref, out_ref, cross_ref):
    slots = out_ref.shape[0] * out_ref.shape[1]
    near_share = near_rows_ref.shape[1] * own_ref.shape[0] // slots
    slot_rows(correlated(near_rows_ref, own_ref, table_ref, cross_ref), out_ref, 0, near_share)
    out_ref[:, :, near_share:, :] = jnp.zeros(
        out_ref.shape[:2] + (out_ref.shape[2] - near_share, out_ref.shape[3]), jnp.float32
    )


def passed_kernel(
    near_rows_ref, passed_ref, far_rows_ref, far_cols_ref, table_ref, count_ref, after_ref,
    out_ref, near_cross_ref, far_cross_ref,
):
    slots = out_ref.shape[0] * out_ref.shape[1]
    near_share = near_rows_ref.shape[1] * passed_ref.shape[0] // slots
    far_share = far_rows_ref.shape[1] * far_cols_ref.shape[0] // slots
    result = correlated(near_rows_ref, passed_ref, table_ref, near_cross_ref)
    slot_rows(result, out_ref, 0, near_share)
    result = correlated(far_rows_ref, far_cols_ref, table_ref, far_cross_ref)
    slot_rows(result, out_ref, near_share, far_share)
    out_ref[:, :, near_share + far_share :, :] = count_ref[...]


def slot_array(kernel, inputs, in_specs, hour_devices, row_total, lag_count, scratch):
    steps = STACK_STEPS
    minor = HOUR_SPLIT[-1]
    major = hour_devices // minor
    return pl.pallas_call(
        kernel,
        grid=(steps,),
        in_specs=in_specs,
        out_specs=pl.BlockSpec((minor, major // steps, row_total, lag_count), lambda i: (0, i, 0, 0)),
        out_shape=jax.ShapeDtypeStruct((minor, major, row_total, lag_count), jnp.float32),
        scratch_shapes=scratch,
    )(*inputs)


def own_slots(white, table, hour_devices, row_total):
    trace_count, wide = white.shape
    lag_count = table.shape[1]
    near_step = trace_count // STACK_STEPS
    full = lambda i: (0, 0)
    in_specs = [
        pl.BlockSpec((1, near_step, wide), lambda i: (i, 0, 0)),
        pl.BlockSpec((trace_count, wide), full),
        pl.BlockSpec((wide, lag_count), full),
    ]
    inputs = (white.reshape(STACK_STEPS, near_step, wide), white, table)
    scratch = [pltpu.VMEM((near_step * trace_count, wide), jnp.bfloat16)]
    return slot_array(own_kernel, inputs, in_specs, hour_devices, row_total, lag_count, scratch)


def passed_slots(white, passed, far_rows, far_cols, table, count_tail, after, hour_devices, row_total):
    trace_count, wide = white.shape
    half_width = far_rows.shape[0]
    lag_count = table.shape[1]
    near_step = trace_count // STACK_STEPS
    far_step = half_width // STACK_STEPS
    minor = HOUR_SPLIT[-1]
    slots = hour_devices // STACK_STEPS
    full = lambda i: (0, 0)
    in_specs = [
        pl.BlockSpec((1, near_step, wide), lambda i: (i, 0, 0)),
        pl.BlockSpec((trace_count, wide), full),
        pl.BlockSpec((1, far_step, wide), lambda i: (i, 0, 0)),
        pl.BlockSpec((trace_count, wide), full),
        pl.BlockSpec((wide, lag_count), full),
        pl.BlockSpec((minor, slots // minor) + count_tail.shape[2:], lambda i: (0, i, 0, 0)),
        pl.BlockSpec(memory_space=pl.ANY),
    ]
    inputs = (
        white.reshape(STACK_STEPS, near_step, wide), passed,
        far_rows.reshape(STACK_STEPS, far_step, wide), far_cols, table, count_tail, after,
    )
    scratch = [
        pltpu.VMEM((near_step * trace_count, wide), jnp.bfloat16),
        pltpu.VMEM((far_step * trace_count, wide), jnp.bfloat16),
    ]
    return slot_array(passed_kernel, inputs, in_specs, hour_devices, row_total, lag_count, scratch)


def core_swap(block):
    core = lax.axis_index("core")
    kept = lax.dynamic_index_in_dim(block, core, 0, keepdims=False)
    sent = lax.dynamic_index_in_dim(block, 1 - core, 0, keepdims=False)
    return kept + lax.ppermute(sent, "core", [(0, 1), (1, 0)])


def on_device(spectra, validity):
    _, station_count, comp_count, part_count, freq_count = spectra.shape
    trace_count = station_count * comp_count
    half_width = trace_count // 2
    wide = part_count * freq_count
    white = whiten(spectra, validity, BAND).reshape(trace_count, wide)
    table = build_table(freq_count, LAGS)
    valid_wire = validity.astype(jnp.bfloat16)
    block_count = lax.axis_size("blocks")
    near_rounds = block_count // 2
    my_block = lax.axis_index("blocks")
    is_lower = my_block < near_rounds
    panels = [(white, valid_wire)]
    for round_index in range(1, near_rounds + 1):
        panels.append(passed_along((white, valid_wire), "blocks", round_index))
    far_white, far_valid = panels[near_rounds]
    far_rows = jnp.where(is_lower, white[:half_width], far_white[half_width:])
    far_cols = jnp.where(is_lower, far_white, white)

    def trace_valid(valid):
        return jnp.repeat(valid.reshape(-1).astype(jnp.float32), comp_count)

    own_valid = trace_valid(valid_wire)
    near_pairs = jnp.stack(
        [
            (own_valid[:, None] * trace_valid(panels[round_index][1])[None, :]).reshape(-1)
            for round_index in range(near_rounds)
        ],
        0,
    )
    far_trace_valid = trace_valid(far_valid)
    far_row_valid = jnp.where(is_lower, own_valid[:half_width], far_trace_valid[half_width:])
    far_col_valid = jnp.where(is_lower, far_trace_valid, own_valid)
    far_pairs = (far_row_valid[:, None] * far_col_valid[None, :]).reshape(-1)

    hour_devices = math.prod(HOUR_SPLIT)
    share_near = trace_count * trace_count // hour_devices
    share_far = half_width * trace_count // hour_devices
    lag_count = table.shape[1]
    count_slots = jnp.concatenate(
        [
            near_pairs.reshape(near_rounds, hour_devices, share_near).transpose(1, 0, 2).reshape(hour_devices, -1),
            far_pairs.reshape(hour_devices, share_far),
        ],
        1,
    )
    row_count = near_rounds * share_near + share_far
    first_rows = -(-share_near // 8) * 8
    rest_rows = -(-(row_count - share_near + 1) // 8) * 8
    count_tail = jnp.zeros((hour_devices, rest_rows - row_count + share_near, lag_count), jnp.float32)
    count_tail = count_tail.at[:, 0, :row_count].set(count_slots)
    minor = HOUR_SPLIT[-1]
    count_tail = count_tail.reshape((hour_devices // minor, minor) + count_tail.shape[1:])
    count_tail = count_tail.transpose(1, 0, 2, 3)
    own = own_slots(white, table, hour_devices, first_rows)
    first = core_swap(own)
    rest = passed_slots(white, panels[1][0], far_rows, far_cols, table, count_tail, own, hour_devices, rest_rows)
    total = jnp.concatenate([first, core_swap(rest)], 1)
    total = total.reshape((HOUR_SPLIT[0], -1) + total.shape[1:]).astype(jnp.bfloat16)
    incoming = lax.all_to_all(total, ("x", "y"), 1, 1, tiled=True)
    total = jnp.sum(incoming.astype(jnp.float32), axis=1)
    upper = lax.axis_index("z_hi") > 0
    kept = jnp.where(upper, total[1], total[0])
    sent = jnp.where(upper, total[0], total[1])
    total = kept + lax.ppermute(sent, "z_hi", [(0, 1), (1, 0)])
    count_at = first_rows + row_count - share_near
    pair_counts = jnp.maximum(total[count_at, :row_count], 1.0)
    first_stack = total[:share_near] / pair_counts[:share_near, None]
    rest_stack = total[first_rows:count_at] / pair_counts[share_near:, None]
    near_stack = jnp.concatenate([first_stack, rest_stack[: (near_rounds - 1) * share_near]], 0)
    near_stack = near_stack.reshape(near_rounds, share_near, lag_count)
    far_stack = rest_stack[(near_rounds - 1) * share_near :]
    return (near_stack[None], far_stack[None])


def solution(mesh):
    hour_mesh = Mesh(
        mesh.devices.reshape(HOUR_SPLIT + (mesh.shape["blocks"],)), HOUR_AXES + ("blocks",)
    )
    in_specs = (P(HOUR_AXES, "blocks", None, None, None), P(HOUR_AXES, "blocks"))
    out_specs = (P("blocks", None, HOUR_AXES, None), P("blocks", HOUR_AXES, None))
    return jax.shard_map(
        on_device, mesh=hour_mesh, in_specs=in_specs, out_specs=out_specs, check_vma=False
    )
```

```python
import math

import jax
import jax.numpy as jnp
from jax import lax
from jax.experimental import pallas as pl
from jax.experimental.pallas import tpu as pltpu
from jax.sharding import Mesh, PartitionSpec as P


BAND = 128
LAGS = 256


EPSILON = 1e-06


HOUR_AXES = ("z_hi", "x", "y", "core")
HOUR_SPLIT = (2, 4, 4, 2)
STACK_STEPS = 4


def passed_along(block, axis, distance):
    devices = range(lax.axis_size(axis))
    route = [((i - distance) % len(devices), i) for i in devices]
    return lax.ppermute(block, axis, route)


def whiten(spectra, validity, band_width):
    hour_count, station_count, comp_count, part_count, freq_count = spectra.shape
    grouped = spectra.reshape(
        hour_count, station_count, comp_count, part_count, freq_count // band_width, band_width
    )
    band_power = jnp.mean(grouped * grouped, axis=(3, 5), keepdims=True)
    valid_f = validity.astype(jnp.float32).reshape(hour_count, station_count, 1, 1, 1, 1)
    scaled = grouped * (valid_f / jnp.sqrt(band_power + EPSILON))
    return scaled.reshape(hour_count, station_count * comp_count, part_count, freq_count).astype(
        jnp.bfloat16
    )


def build_table(freq_count, lag_count):
    fine_count = 64
    coarse_count = freq_count // fine_count
    lag_index = jnp.arange(lag_count, dtype=jnp.int32)[None, :] - lag_count // 2
    period = 2 * freq_count

    def angle_of(freq_index):
        residue = freq_index[:, None] * (lag_index + period) % period
        return residue.astype(jnp.float32) * (math.pi / freq_count)

    coarse = angle_of(jnp.arange(coarse_count, dtype=jnp.int32) * fine_count)[:, None, :]
    fine = angle_of(jnp.arange(fine_count, dtype=jnp.int32))[None, :, :]
    coarse_cos, coarse_sin = jnp.cos(coarse), jnp.sin(coarse)
    fine_cos, fine_sin = jnp.cos(fine), jnp.sin(fine)
    cos_part = (coarse_cos * fine_cos - coarse_sin * fine_sin).reshape(freq_count, lag_count)
    sin_part = (coarse_sin * fine_cos + coarse_cos * fine_sin).reshape(freq_count, lag_count)
    amplitude = 8.0 / math.sqrt(freq_count)
    return jnp.concatenate([cos_part * amplitude, -sin_part * amplitude], 0).astype(jnp.bfloat16)


def cross_into(rows_ref, cols_ref, cross_ref):
    row_step = rows_ref.shape[1]
    col_count, wide = cols_ref.shape
    freq_count = wide // 2
    chunk = 256
    for start in range(0, freq_count, chunk):
        col_real = cols_ref[:, start : start + chunk].astype(jnp.float32)
        col_imag = cols_ref[:, freq_count + start : freq_count + start + chunk].astype(jnp.float32)
        for row in range(row_step):
            row_real = rows_ref[0, row : row + 1, start : start + chunk].astype(jnp.float32)
            row_imag = rows_ref[0, row : row + 1, freq_count + start : freq_count + start + chunk]
            row_imag = row_imag.astype(jnp.float32)
            real_part = row_real * col_real + row_imag * col_imag
            imag_part = row_imag * col_real - row_real * col_imag
            first = row * col_count
            cross_ref[first : first + col_count, start : start + chunk] = real_part.astype(jnp.bfloat16)
            cross_ref[first : first + col_count, freq_count + start : freq_count + start + chunk] = (
                imag_part.astype(jnp.bfloat16)
            )


def slot_rows(result, out_ref, offset, share):
    minor, major = out_ref.shape[:2]
    for slot in range(minor * major):
        out_ref[slot % minor, slot // minor, offset : offset + share, :] = result[
            slot * share : (slot + 1) * share
        ]


def correlated(rows_ref, cols_ref, table_ref, cross_ref):
    cross_into(rows_ref, cols_ref, cross_ref)
    return jnp.dot(cross_ref[...], table_ref[...], preferred_element_type=jnp.float32)


def own_kernel(near_rows_ref, own_ref, table_ref, out_ref, cross_ref):
    slots = out_ref.shape[0] * out_ref.shape[1]
    near_share = near_rows_ref.shape[1] * own_ref.shape[0] // slots
    slot_rows(correlated(near_rows_ref, own_ref, table_ref, cross_ref), out_ref, 0, near_share)
    out_ref[:, :, near_share:, :] = jnp.zeros(
        out_ref.shape[:2] + (out_ref.shape[2] - near_share, out_ref.shape[3]), jnp.float32
    )


def passed_kernel(
    near_rows_ref, passed_ref, far_rows_ref, far_cols_ref, table_ref, count_ref, after_ref,
    out_ref, near_cross_ref, far_cross_ref,
):
    slots = out_ref.shape[0] * out_ref.shape[1]
    near_share = near_rows_ref.shape[1] * passed_ref.shape[0] // slots
    far_share = far_rows_ref.shape[1] * far_cols_ref.shape[0] // slots
    result = correlated(near_rows_ref, passed_ref, table_ref, near_cross_ref)
    slot_rows(result, out_ref, 0, near_share)
    result = correlated(far_rows_ref, far_cols_ref, table_ref, far_cross_ref)
    slot_rows(result, out_ref, near_share, far_share)
    out_ref[:, :, near_share + far_share :, :] = count_ref[...]


def slot_array(kernel, inputs, in_specs, hour_devices, row_total, lag_count, scratch):
    steps = STACK_STEPS
    minor = HOUR_SPLIT[-1]
    major = hour_devices // minor
    return pl.pallas_call(
        kernel,
        grid=(steps,),
        in_specs=in_specs,
        out_specs=pl.BlockSpec((minor, major // steps, row_total, lag_count), lambda i: (0, i, 0, 0)),
        out_shape=jax.ShapeDtypeStruct((minor, major, row_total, lag_count), jnp.float32),
        scratch_shapes=scratch,
    )(*inputs)


def own_slots(white, table, hour_devices, row_total):
    trace_count, wide = white.shape
    lag_count = table.shape[1]
    near_step = trace_count // STACK_STEPS
    full = lambda i: (0, 0)
    in_specs = [
        pl.BlockSpec((1, near_step, wide), lambda i: (i, 0, 0)),
        pl.BlockSpec((trace_count, wide), full),
        pl.BlockSpec((wide, lag_count), full),
    ]
    inputs = (white.reshape(STACK_STEPS, near_step, wide), white, table)
    scratch = [pltpu.VMEM((near_step * trace_count, wide), jnp.bfloat16)]
    return slot_array(own_kernel, inputs, in_specs, hour_devices, row_total, lag_count, scratch)


def passed_slots(white, passed, far_rows, far_cols, table, count_tail, after, hour_devices, row_total):
    trace_count, wide = white.shape
    half_width = far_rows.shape[0]
    lag_count = table.shape[1]
    near_step = trace_count // STACK_STEPS
    far_step = half_width // STACK_STEPS
    minor = HOUR_SPLIT[-1]
    slots = hour_devices // STACK_STEPS
    full = lambda i: (0, 0)
    in_specs = [
        pl.BlockSpec((1, near_step, wide), lambda i: (i, 0, 0)),
        pl.BlockSpec((trace_count, wide), full),
        pl.BlockSpec((1, far_step, wide), lambda i: (i, 0, 0)),
        pl.BlockSpec((trace_count, wide), full),
        pl.BlockSpec((wide, lag_count), full),
        pl.BlockSpec((minor, slots // minor) + count_tail.shape[2:], lambda i: (0, i, 0, 0)),
        pl.BlockSpec(memory_space=pl.ANY),
    ]
    inputs = (
        white.reshape(STACK_STEPS, near_step, wide), passed,
        far_rows.reshape(STACK_STEPS, far_step, wide), far_cols, table, count_tail, after,
    )
    scratch = [
        pltpu.VMEM((near_step * trace_count, wide), jnp.bfloat16),
        pltpu.VMEM((far_step * trace_count, wide), jnp.bfloat16),
    ]
    return slot_array(passed_kernel, inputs, in_specs, hour_devices, row_total, lag_count, scratch)


def core_swap(block):
    core = lax.axis_index("core")
    kept = lax.dynamic_index_in_dim(block, core, 0, keepdims=False)
    sent = lax.dynamic_index_in_dim(block, 1 - core, 0, keepdims=False)
    return kept + lax.ppermute(sent, "core", [(0, 1), (1, 0)])


def on_device(spectra, validity):
    _, station_count, comp_count, part_count, freq_count = spectra.shape
    trace_count = station_count * comp_count
    half_width = trace_count // 2
    wide = part_count * freq_count
    white = whiten(spectra, validity, BAND).reshape(trace_count, wide)
    table = build_table(freq_count, LAGS)
    valid_wire = validity.astype(jnp.bfloat16)
    block_count = lax.axis_size("blocks")
    near_rounds = block_count // 2
    my_block = lax.axis_index("blocks")
    is_lower = my_block < near_rounds
    valid_rows = jnp.zeros((8, wide), jnp.bfloat16).at[0, :station_count].set(valid_wire.reshape(-1))
    packed = jnp.concatenate([white, valid_rows], 0)
    panels = [(white, valid_wire)]
    for round_index in range(1, near_rounds + 1):
        panel = passed_along(packed, "blocks", round_index)
        panels.append((panel[:trace_count], panel[trace_count, :station_count]))
    far_white, far_valid = panels[near_rounds]
    far_rows = jnp.where(is_lower, white[:half_width], far_white[half_width:])
    far_cols = jnp.where(is_lower, far_white, white)

    def trace_valid(valid):
        return jnp.repeat(valid.reshape(-1).astype(jnp.float32), comp_count)

    own_valid = trace_valid(valid_wire)
    near_pairs = jnp.stack(
        [
            (own_valid[:, None] * trace_valid(panels[round_index][1])[None, :]).reshape(-1)
            for round_index in range(near_rounds)
        ],
        0,
    )
    far_trace_valid = trace_valid(far_valid)
    far_row_valid = jnp.where(is_lower, own_valid[:half_width], far_trace_valid[half_width:])
    far_col_valid = jnp.where(is_lower, far_trace_valid, own_valid)
    far_pairs = (far_row_valid[:, None] * far_col_valid[None, :]).reshape(-1)

    hour_devices = math.prod(HOUR_SPLIT)
    share_near = trace_count * trace_count // hour_devices
    share_far = half_width * trace_count // hour_devices
    lag_count = table.shape[1]
    count_slots = jnp.concatenate(
        [
            near_pairs.reshape(near_rounds, hour_devices, share_near).transpose(1, 0, 2).reshape(hour_devices, -1),
            far_pairs.reshape(hour_devices, share_far),
        ],
        1,
    )
    row_count = near_rounds * share_near + share_far
    first_rows = -(-share_near // 8) * 8
    rest_rows = -(-(row_count - share_near + 1) // 8) * 8
    count_tail = jnp.zeros((hour_devices, rest_rows - row_count + share_near, lag_count), jnp.float32)
    count_tail = count_tail.at[:, 0, :row_count].set(count_slots)
    minor = HOUR_SPLIT[-1]
    count_tail = count_tail.reshape((hour_devices // minor, minor) + count_tail.shape[1:])
    count_tail = count_tail.transpose(1, 0, 2, 3)
    own = own_slots(white, table, hour_devices, first_rows)
    first = core_swap(own)
    rest = passed_slots(white, panels[1][0], far_rows, far_cols, table, count_tail, own, hour_devices, rest_rows)
    total = jnp.concatenate([first, core_swap(rest)], 1)
    total = total.reshape((HOUR_SPLIT[0], -1) + total.shape[1:]).astype(jnp.bfloat16)
    incoming = lax.all_to_all(total, ("x", "y"), 1, 1, tiled=True)
    total = jnp.sum(incoming.astype(jnp.float32), axis=1)
    upper = lax.axis_index("z_hi") > 0
    kept = jnp.where(upper, total[1], total[0])
    sent = jnp.where(upper, total[0], total[1])
    total = kept + lax.ppermute(sent, "z_hi", [(0, 1), (1, 0)])
    count_at = first_rows + row_count - share_near
    pair_counts = jnp.maximum(total[count_at, :row_count], 1.0)
    first_stack = total[:share_near] / pair_counts[:share_near, None]
    rest_stack = total[first_rows:count_at] / pair_counts[share_near:, None]
    near_stack = jnp.concatenate([first_stack, rest_stack[: (near_rounds - 1) * share_near]], 0)
    near_stack = near_stack.reshape(near_rounds, share_near, lag_count)
    far_stack = rest_stack[(near_rounds - 1) * share_near :]
    return (near_stack[None], far_stack[None])


def solution(mesh):
    hour_mesh = Mesh(
        mesh.devices.reshape(HOUR_SPLIT + (mesh.shape["blocks"],)), HOUR_AXES + ("blocks",)
    )
    in_specs = (P(HOUR_AXES, "blocks", None, None, None), P(HOUR_AXES, "blocks"))
    out_specs = (P("blocks", None, HOUR_AXES, None), P("blocks", HOUR_AXES, None))
    return jax.shard_map(
        on_device, mesh=hour_mesh, in_specs=in_specs, out_specs=out_specs, check_vma=False
    )
```
